256 devices in a mesh: rows: 64 (over y, z, core), freq: 4 (over x).
Axes of the slice: x: 4, y: 4, z: 8, core: 2. Of those that a mesh axis runs over, the one named last changes fastest.
Arguments:
- snapshots: bfloat16 [1048576, 512], P('rows', 'freq'), may hold values from -60 to 60
- block_cols: int32 [8192, 3], P('rows'), may hold values from 0 to 8191, as said below
- mass_blocks: bfloat16 [8192, 3, 128, 128], P('rows'), may hold values from -2 to 2
- start_group: float32 [512, 32], P('freq'), may hold values from -6 to 6
- start_merge: float32 [64, 32], replicated, may hold values from -6 to 6
Outputs:
- modes: float32 [32, 1048576], P(None, ('rows', 'freq'))
The draws below stay inside these ranges and needn't reach their ends.
Inputs may be any that keep to these rules, and one draw needn't show every extreme that they name: block_cols[b, 0] is b; the other entries lie within 2 of b, differ from b, and may repeat near the ends.
All inputs are finite; a program needn't handle non-finite values.
Results may differ from the reference program's by a relative error of at most 0.0003.
Values may be sent and summed in bfloat16 or wider, within the bound.
No kernel may reach another device: no remote copies, remote signals or barrier semaphores. Data moves between devices by JAX's collectives and lax.ppermute only.
A program may use at most 128 MiB of HBM per device.

```python
import math
import jax
import jax.numpy as jnp
from jax import lax

BLK = 128
KB = 3
HB = 2
COLS = 512
RANK = 32
POWER = 2
COLS_DEV = 128
NB = 8192
NROWS = 1048576
LEVELS = 2
N_FREQ = 4


def draw_snapshots(key, part):
    basis_key, mixing_key, noise_key, column_key, row_key, wave_key, phase_key, depth_key = jax.random.split(key, 8)
    shared_rank = 64
    position = (jnp.arange(NROWS, dtype=jnp.float32) + 0.5) / NROWS
    waves = jax.random.randint(wave_key, (1, shared_rank), 1, 4).astype(jnp.float32)
    phases = jax.random.uniform(phase_key, (1, shared_rank), jnp.float32, 0.0, 2.0 * math.pi)
    depth = jax.random.uniform(depth_key, (1, shared_rank), jnp.float32, 0.3, 1.0)
    envelope = jnp.exp(depth * jnp.sin(2.0 * math.pi * waves * position[:, None] + phases))
    trend = jnp.exp(math.log(3.0) * position)[:, None]
    mode_index = jnp.arange(shared_rank, dtype=jnp.float32)
    basis = jax.random.normal(basis_key, (NROWS, shared_rank), jnp.float32)
    mixing = jax.random.normal(mixing_key, (shared_rank, COLS), jnp.float32)
    noise = jax.random.normal(noise_key, (NROWS, COLS), jnp.float32)
    decay = 1.0 / (1.0 + mode_index / 16.0)
    column_scale = jnp.exp(jax.random.uniform(column_key, (1, COLS), jnp.float32, math.log(0.3), math.log(3.0)))
    row_scale = jnp.exp(jax.random.uniform(row_key, (NROWS, 1), jnp.float32, math.log(0.5), math.log(2.0)))
    decay = decay / jnp.sqrt(jnp.sum(decay * decay))
    shared = jnp.dot(basis * envelope * decay[None, :], mixing, precision=lax.Precision.HIGHEST)
    values = 0.2 * (shared + 0.4 * noise) * column_scale * row_scale * trend
    return jnp.clip(values, -60.0, 60.0).astype(jnp.bfloat16)


def draw_block_cols(key, part):
    scores = jax.random.randint(key, (NB, 2 * HB), 0, 1 << 20) * (2 * HB) + jnp.arange(2 * HB)
    ordering = jnp.argsort(scores, axis=1)
    choices_table = jnp.concatenate([-jnp.arange(HB, 0, -1), jnp.arange(1, HB + 1)])
    offsets = choices_table[ordering[:, :KB - 1]]
    own_block = jnp.arange(NB)[:, None]
    target = own_block + offsets
    target = jnp.where((target < 0) | (target >= NB), own_block - offsets, target)
    return jnp.concatenate([own_block, target], axis=1).astype(jnp.int32)


def draw_mass_blocks(key, part):
    values = jax.random.normal(key, (NB, KB, BLK, BLK), jnp.float32)
    is_diagonal = (jnp.arange(KB) == 0)[None, :, None, None]
    spread = jnp.where(is_diagonal, 0.3, 0.5) / math.sqrt(BLK)
    identity_part = jnp.where(is_diagonal, jnp.eye(BLK, dtype=jnp.float32)[None, None], 0.0)
    return jnp.clip(identity_part + spread * values, -2.0, 2.0).astype(jnp.bfloat16)


def block_levels(stream_key, shape, shards, smallest, largest):
    def one(dim, blocks):
        steps = jax.random.uniform(jax.random.fold_in(jax.random.fold_in(stream_key, 6), dim), (blocks,), jnp.float32, smallest / len(shards), largest / len(shards))
        return jnp.repeat(jnp.exp(steps), shape[dim] // blocks).reshape((-1,) + (1,) * (len(shape) - dim - 1))

    loudness = one(*shards[0])
    for cut in shards[1:]:
        loudness = loudness * one(*cut)
    return loudness


def scatter_about(own_key, extent, scale, limit, cuts=(), kind=jnp.bfloat16):
    entries = scale * jax.random.normal(own_key, extent, jnp.float32)
    if cuts:
        entries = entries * block_levels(own_key, extent, cuts, -0.22, 0.18)
    return jnp.clip(entries, -limit, limit).astype(kind)


def setup_inputs(seed: int = 0) -> dict:
    seeds = jax.random.split(jax.random.key(seed), 6)
    return {
        "snapshots": draw_snapshots(jax.random.fold_in(seeds[5], 71), 0),
        "block_cols": draw_block_cols(jax.random.fold_in(seeds[5], 71), 0),
        "mass_blocks": draw_mass_blocks(jax.random.fold_in(seeds[5], 71), 0),
        "start_group": scatter_about(seeds[3], (COLS, RANK), 1.0, 6.0, ((0, 4),), jnp.float32),
        "start_merge": scatter_about(seeds[4], (2 * RANK, RANK), 1.0, 6.0, (), jnp.float32),
    }


HIGHEST = lax.Precision.HIGHEST

def orthonormal(columns_block):
    inner_gram = jnp.dot(columns_block.T, columns_block, precision=HIGHEST)
    lower_factor = jnp.linalg.cholesky(inner_gram)
    return lax.linalg.triangular_solve(lower_factor, columns_block, left_side=False, lower=True, transpose_a=True)

def subspace(gram_matrix, start_block):
    current = start_block
    for repeat in range(POWER):
        current = orthonormal(jnp.dot(gram_matrix, current, precision=HIGHEST))
    return current

def apply_mass(snapshots, block_cols, mass_blocks):
    padded = jnp.pad(snapshots, ((HB * BLK, HB * BLK), (0, 0)))
    tile_stack = padded.reshape(NB + 2 * HB, BLK, COLS)

    def one_row(inputs):
        columns, blocks = inputs
        picked = tile_stack[columns + HB].astype(jnp.float32)
        return jnp.einsum('kij,kjc->ic', blocks.astype(jnp.float32), picked, precision=HIGHEST)
    return lax.map(one_row, (block_cols, mass_blocks)).reshape(NB * BLK, COLS)

def reference(snapshots, block_cols, mass_blocks, start_group, start_merge):
    weighted = apply_mass(snapshots, block_cols, mass_blocks)
    nodes = []
    for group_id in range(N_FREQ):
        part_cols = weighted[:, group_id * COLS_DEV:(group_id + 1) * COLS_DEV]
        group_gram = jnp.dot(part_cols.T, part_cols, precision=HIGHEST) / NROWS
        weights = subspace(group_gram, start_group[group_id * COLS_DEV:(group_id + 1) * COLS_DEV])
        nodes.append(jnp.dot(weights.T, part_cols.T, precision=HIGHEST))
    for section_index in range(LEVELS):
        merged = []
        for position in range(0, len(nodes), 2):
            joined = jnp.concatenate([nodes[position], nodes[position + 1]], axis=0)
            pair_gram = jnp.dot(joined, joined.T, precision=HIGHEST) / NROWS
            merged.append(jnp.dot(subspace(pair_gram, start_merge).T, joined, precision=HIGHEST))
        nodes = merged
    return nodes[0]
```

```python
import jax
import jax.numpy as jnp
from jax import lax
from jax.sharding import PartitionSpec as P

HB = 2
POWER = 2


HIGHEST = lax.Precision.HIGHEST


def extended_2(block, sides, width):
    for axis, dim in sides:
        count = lax.axis_size(axis)
        forward = [(i, i + 1) for i in range(count - 1)]
        backward = [(target, source) for source, target in forward]
        low = lax.ppermute(
            lax.slice_in_dim(block, block.shape[dim] - width, None, axis=dim), axis, forward
        )
        high = lax.ppermute(lax.slice_in_dim(block, 0, width, axis=dim), axis, backward)
        block = jnp.concatenate([low, block, high], axis=dim)
    return block


def orthonormal(columns_block):
    inner_gram = jnp.dot(columns_block.T, columns_block, precision=HIGHEST)
    lower_factor = jnp.linalg.cholesky(inner_gram)
    return lax.linalg.triangular_solve(
        lower_factor, columns_block, left_side=False, lower=True, transpose_a=True
    )


def subspace(gram_matrix, start_block):
    current = start_block
    for repeat in range(POWER):
        current = orthonormal(jnp.dot(gram_matrix, current, precision=HIGHEST))
    return current


def coefficient_tree(full_gram, start_merge, rank_size, freq_count):
    pairs = freq_count // 2
    width = 2 * rank_size
    blocks = jnp.stack(
        [full_gram[p * width : (p + 1) * width, p * width : (p + 1) * width] for p in range(pairs)]
    )
    pair_weights = jax.vmap(subspace, in_axes=(0, None))(blocks, start_merge)
    zero = jnp.zeros((width, rank_size), jnp.float32)
    coefficients = []
    for p in range(pairs):
        parts = [zero] * pairs
        parts[p] = pair_weights[p]
        coefficients.append(jnp.concatenate(parts, axis=0))
    while len(coefficients) > 1:
        merged = []
        for position in range(0, len(coefficients), 2):
            joined = jnp.concatenate([coefficients[position], coefficients[position + 1]], axis=1)
            pair_gram = jnp.dot(
                joined.T, jnp.dot(full_gram, joined, precision=HIGHEST), precision=HIGHEST
            )
            merged.append(jnp.dot(joined, subspace(pair_gram, start_merge), precision=HIGHEST))
        coefficients = merged
    return coefficients[0]


def shards(snapshots, block_cols, mass_blocks, start_group, start_merge):
    block_size = mass_blocks.shape[2]
    local_blocks = block_cols.shape[0]
    local_cols = snapshots.shape[1]
    total_rows = lax.axis_size("rows") * snapshots.shape[0]
    extended = extended_2(snapshots, (("rows", 0),), HB * block_size)
    tile_stack = extended.reshape(local_blocks + 2 * HB, block_size, local_cols)
    local_index = block_cols - lax.axis_index("rows") * local_blocks + HB
    picked = tile_stack[local_index]
    weighted = jnp.einsum("bkij,bkjc->bic", mass_blocks, picked, preferred_element_type=jnp.float32)
    weighted = weighted.reshape(local_blocks * block_size, local_cols)
    local_gram = jnp.dot(weighted.T, weighted, precision=HIGHEST)
    group_gram = lax.psum(local_gram, "rows") / total_rows
    weights = subspace(group_gram, start_group)
    modes = lax.dot_general(weights, weighted, (((0,), (1,)), ((), ())), precision=HIGHEST)
    rank_size = modes.shape[0]
    freq_count = lax.axis_size("freq")
    quarter = lax.all_to_all(modes, "freq", 1, 0, tiled=True)
    full_gram = (
        lax.psum(jnp.dot(quarter, quarter.T, precision=HIGHEST), ("rows", "freq")) / total_rows
    )
    combined = coefficient_tree(full_gram, start_merge, rank_size, freq_count)
    result = jnp.dot(combined.T, quarter, precision=HIGHEST)
    return result


def solution(mesh):
    in_specs = (
        P("rows", "freq"),
        P("rows", None),
        P("rows", None, None, None),
        P("freq", None),
        P(),
    )
    out_specs = P(None, ("rows", "freq"))
    return jax.shard_map(shards, mesh=mesh, in_specs=in_specs, out_specs=out_specs, check_vma=False)
```

```python
import jax
import jax.numpy as jnp
from jax import lax
from jax.sharding import PartitionSpec as P

HB = 2
POWER = 2


HIGHEST = lax.Precision.HIGHEST


def extended_2(block, sides, width):
    for axis, dim in sides:
        count = lax.axis_size(axis)
        forward = [(i, i + 1) for i in range(count - 1)]
        backward = [(target, source) for source, target in forward]
        low = lax.ppermute(
            lax.slice_in_dim(block, block.shape[dim] - width, None, axis=dim), axis, forward
        )
        high = lax.ppermute(lax.slice_in_dim(block, 0, width, axis=dim), axis, backward)
        block = jnp.concatenate([low, block, high], axis=dim)
    return block


def butterfly_sum(x, axes):
    for axis in axes:
        count = lax.axis_size(axis)
        step = 1
        while step < count:
            pairs = [(i, i ^ step) for i in range(count)]
            x = x + lax.ppermute(x, axis, pairs)
            step *= 2
    return x


def orthonormal(columns_block):
    inner_gram = jnp.dot(columns_block.T, columns_block, precision=HIGHEST)
    lower_factor = jnp.linalg.cholesky(inner_gram)
    return lax.linalg.triangular_solve(
        lower_factor, columns_block, left_side=False, lower=True, transpose_a=True
    )


def subspace(gram_matrix, start_block):
    current = start_block
    for repeat in range(POWER):
        current = orthonormal(jnp.dot(gram_matrix, current, precision=HIGHEST))
    return current


def coefficient_tree(full_gram, start_merge, rank_size, freq_count):
    pairs = freq_count // 2
    width = 2 * rank_size
    blocks = jnp.stack(
        [full_gram[p * width : (p + 1) * width, p * width : (p + 1) * width] for p in range(pairs)]
    )
    pair_weights = jax.vmap(subspace, in_axes=(0, None))(blocks, start_merge)
    zero = jnp.zeros((width, rank_size), jnp.float32)
    coefficients = []
    for p in range(pairs):
        parts = [zero] * pairs
        parts[p] = pair_weights[p]
        coefficients.append(jnp.concatenate(parts, axis=0))
    while len(coefficients) > 1:
        merged = []
        for position in range(0, len(coefficients), 2):
            joined = jnp.concatenate([coefficients[position], coefficients[position + 1]], axis=1)
            pair_gram = jnp.dot(
                joined.T, jnp.dot(full_gram, joined, precision=HIGHEST), precision=HIGHEST
            )
            merged.append(jnp.dot(joined, subspace(pair_gram, start_merge), precision=HIGHEST))
        coefficients = merged
    return coefficients[0]


def shards(snapshots, block_cols, mass_blocks, start_group, start_merge):
    block_size = mass_blocks.shape[2]
    local_blocks = block_cols.shape[0]
    local_cols = snapshots.shape[1]
    total_rows = lax.axis_size("rows") * snapshots.shape[0]
    extended = extended_2(snapshots, (("rows", 0),), HB * block_size)
    tile_stack = extended.reshape(local_blocks + 2 * HB, block_size, local_cols)
    local_index = block_cols - lax.axis_index("rows") * local_blocks + HB
    picked = tile_stack[local_index]
    weighted = jnp.einsum("bkij,bkjc->bic", mass_blocks, picked, preferred_element_type=jnp.float32)
    weighted = weighted.reshape(local_blocks * block_size, local_cols)
    local_gram = jnp.dot(weighted.T, weighted, precision=HIGHEST)
    group_gram = butterfly_sum(local_gram, ("rows",)) / total_rows
    weights = subspace(group_gram, start_group)
    modes = lax.dot_general(weights, weighted, (((0,), (1,)), ((), ())), precision=HIGHEST)
    rank_size = modes.shape[0]
    freq_count = lax.axis_size("freq")
    group = lax.axis_index("freq")
    share = modes.shape[1] // freq_count
    received = [lax.dynamic_slice_in_dim(modes, group * share, share, 1)]
    for shift in range(1, freq_count):
        piece = lax.dynamic_slice_in_dim(modes, ((group + shift) % freq_count) * share, share, 1)
        pairs = [(i, (i + shift) % freq_count) for i in range(freq_count)]
        received.append(lax.ppermute(piece, "freq", pairs))
    stacked = jnp.concatenate(received, axis=0)
    source = (group - jnp.arange(freq_count)) % freq_count
    local_full = jnp.dot(stacked, stacked.T, precision=HIGHEST)
    blocked = local_full.reshape(freq_count, rank_size, freq_count, rank_size)
    blocked = jnp.take(jnp.take(blocked, source, axis=0), source, axis=2)
    full_gram = butterfly_sum(
        blocked.reshape(freq_count * rank_size, freq_count * rank_size), ("rows", "freq")
    ) / total_rows
    combined = coefficient_tree(full_gram, start_merge, rank_size, freq_count)
    shifted = jnp.take(combined.reshape(freq_count, rank_size, rank_size), source, axis=0)
    result = jnp.dot(shifted.reshape(freq_count * rank_size, rank_size).T, stacked, precision=HIGHEST)
    return result


def solution(mesh):
    in_specs = (
        P("rows", "freq"),
        P("rows", None),
        P("rows", None, None, None),
        P("freq", None),
        P(),
    )
    out_specs = P(None, ("rows", "freq"))
    return jax.shard_map(shards, mesh=mesh, in_specs=in_specs, out_specs=out_specs, check_vma=False)
```

```python
import jax
import jax.numpy as jnp
from jax import lax
from jax.sharding import PartitionSpec as P
from jax.experimental import pallas as pl
from jax.experimental.pallas import tpu as pltpu

HB = 2
POWER = 2


HIGHEST = lax.Precision.HIGHEST


def extended_2(block, sides, width):
    for axis, dim in sides:
        count = lax.axis_size(axis)
        forward = [(i, i + 1) for i in range(count - 1)]
        backward = [(target, source) for source, target in forward]
        low = lax.ppermute(
            lax.slice_in_dim(block, block.shape[dim] - width, None, axis=dim), axis, forward
        )
        high = lax.ppermute(lax.slice_in_dim(block, 0, width, axis=dim), axis, backward)
        block = jnp.concatenate([low, block, high], axis=dim)
    return block


ROWS_PER_STEP = 16


def mass_kernel(index_ref, low_ref, own_ref, high_ref, mass_ref, out_ref, gram_ref):
    step = pl.program_id(0)
    size = mass_ref.shape[2]
    halo = low_ref.shape[0] // size
    own_tiles = own_ref.shape[0] // size
    rows_here = mass_ref.shape[0]
    kb = mass_ref.shape[1]

    @pl.when(step == 0)
    def _():
        gram_ref[...] = jnp.zeros(gram_ref.shape, gram_ref.dtype)

    for row in range(rows_here):
        block = step * rows_here + row
        total = jnp.zeros((size, out_ref.shape[1]), jnp.float32)
        for k in range(kb):
            tile_id = index_ref[block * kb + k]
            own_at = jnp.clip(tile_id - halo, 0, own_tiles - 1)
            low_at = jnp.clip(tile_id, 0, halo - 1)
            high_at = jnp.clip(tile_id - halo - own_tiles, 0, halo - 1)
            own_tile = own_ref[pl.ds(pl.multiple_of(own_at * size, size), size), :]
            low_tile = low_ref[pl.ds(pl.multiple_of(low_at * size, size), size), :]
            high_tile = high_ref[pl.ds(pl.multiple_of(high_at * size, size), size), :]
            tile = jnp.where(
                tile_id < halo, low_tile, jnp.where(tile_id >= halo + own_tiles, high_tile, own_tile)
            )
            total = total + jnp.dot(mass_ref[row, k], tile, preferred_element_type=jnp.float32)
        out_ref[row * size : (row + 1) * size, :] = total

    chunk = out_ref[...]
    high_part = chunk.astype(jnp.bfloat16)
    low_part = (chunk - high_part.astype(jnp.float32)).astype(jnp.bfloat16)
    dims = (((0,), (0,)), ((), ()))
    main = lax.dot_general(high_part, high_part, dims, preferred_element_type=jnp.float32)
    cross = lax.dot_general(high_part, low_part, dims, preferred_element_type=jnp.float32)
    gram_ref[...] += main + (cross + cross.T)


def apply_mass(low, own, high, mass_blocks, tile_index):
    blocks, kb, size, _ = mass_blocks.shape
    cols = own.shape[1]
    per = ROWS_PER_STEP
    grid_spec = pltpu.PrefetchScalarGridSpec(
        num_scalar_prefetch=1,
        grid=(blocks // per,),
        in_specs=[
            pl.BlockSpec(low.shape, lambda i, idx: (0, 0)),
            pl.BlockSpec(own.shape, lambda i, idx: (0, 0)),
            pl.BlockSpec(high.shape, lambda i, idx: (0, 0)),
            pl.BlockSpec((per, kb, size, size), lambda i, idx: (i, 0, 0, 0)),
        ],
        out_specs=[
            pl.BlockSpec((per * size, cols), lambda i, idx: (i, 0)),
            pl.BlockSpec((cols, cols), lambda i, idx: (0, 0)),
        ],
    )
    return pl.pallas_call(
        mass_kernel,
        grid_spec=grid_spec,
        out_shape=[
            jax.ShapeDtypeStruct((blocks * size, cols), jnp.float32),
            jax.ShapeDtypeStruct((cols, cols), jnp.float32),
        ],
        compiler_params=pltpu.CompilerParams(dimension_semantics=("arbitrary",)),
    )(tile_index.reshape(-1), low, own, high, mass_blocks)


def butterfly_sum(x, axes):
    for axis in axes:
        count = lax.axis_size(axis)
        step = 1
        while step < count:
            pairs = [(i, i ^ step) for i in range(count)]
            x = x + lax.ppermute(x, axis, pairs)
            step *= 2
    return x


def orthonormal(columns_block):
    inner_gram = jnp.dot(columns_block.T, columns_block, precision=HIGHEST)
    lower_factor = jnp.linalg.cholesky(inner_gram)
    return lax.linalg.triangular_solve(
        lower_factor, columns_block, left_side=False, lower=True, transpose_a=True
    )


def subspace(gram_matrix, start_block):
    current = start_block
    for repeat in range(POWER):
        current = orthonormal(jnp.dot(gram_matrix, current, precision=HIGHEST))
    return current


def coefficient_tree(full_gram, start_merge, rank_size, freq_count):
    pairs = freq_count // 2
    width = 2 * rank_size
    blocks = jnp.stack(
        [full_gram[p * width : (p + 1) * width, p * width : (p + 1) * width] for p in range(pairs)]
    )
    pair_weights = jax.vmap(subspace, in_axes=(0, None))(blocks, start_merge)
    zero = jnp.zeros((width, rank_size), jnp.float32)
    coefficients = []
    for p in range(pairs):
        parts = [zero] * pairs
        parts[p] = pair_weights[p]
        coefficients.append(jnp.concatenate(parts, axis=0))
    while len(coefficients) > 1:
        merged = []
        for position in range(0, len(coefficients), 2):
            joined = jnp.concatenate([coefficients[position], coefficients[position + 1]], axis=1)
            pair_gram = jnp.dot(
                joined.T, jnp.dot(full_gram, joined, precision=HIGHEST), precision=HIGHEST
            )
            merged.append(jnp.dot(joined, subspace(pair_gram, start_merge), precision=HIGHEST))
        coefficients = merged
    return coefficients[0]


def shards(snapshots, block_cols, mass_blocks, start_group, start_merge):
    block_size = mass_blocks.shape[2]
    local_blocks = block_cols.shape[0]
    local_cols = snapshots.shape[1]
    total_rows = lax.axis_size("rows") * snapshots.shape[0]
    width = HB * block_size
    count = lax.axis_size("rows")
    forward = [(i, i + 1) for i in range(count - 1)]
    backward = [(target, source) for source, target in forward]
    low = lax.ppermute(snapshots[snapshots.shape[0] - width :], "rows", forward)
    high = lax.ppermute(snapshots[:width], "rows", backward)
    local_index = block_cols - lax.axis_index("rows") * local_blocks + HB
    weighted, local_gram = apply_mass(low, snapshots, high, mass_blocks, local_index)
    group_gram = butterfly_sum(local_gram, ("rows",)) / total_rows
    weights = subspace(group_gram, start_group)
    modes = lax.dot_general(weights, weighted, (((0,), (1,)), ((), ())), precision=HIGHEST)
    rank_size = modes.shape[0]
    freq_count = lax.axis_size("freq")
    group = lax.axis_index("freq")
    share = modes.shape[1] // freq_count
    received = [lax.dynamic_slice_in_dim(modes, group * share, share, 1)]
    for shift in range(1, freq_count):
        piece = lax.dynamic_slice_in_dim(modes, ((group + shift) % freq_count) * share, share, 1)
        pairs = [(i, (i + shift) % freq_count) for i in range(freq_count)]
        received.append(lax.ppermute(piece, "freq", pairs))
    stacked = jnp.concatenate(received, axis=0)
    source = (group - jnp.arange(freq_count)) % freq_count
    local_full = jnp.dot(stacked, stacked.T, precision=HIGHEST)
    blocked = local_full.reshape(freq_count, rank_size, freq_count, rank_size)
    blocked = jnp.take(jnp.take(blocked, source, axis=0), source, axis=2)
    full_gram = butterfly_sum(
        blocked.reshape(freq_count * rank_size, freq_count * rank_size), ("rows", "freq")
    ) / total_rows
    combined = coefficient_tree(full_gram, start_merge, rank_size, freq_count)
    shifted = jnp.take(combined.reshape(freq_count, rank_size, rank_size), source, axis=0)
    result = jnp.dot(shifted.reshape(freq_count * rank_size, rank_size).T, stacked, precision=HIGHEST)
    return result


def solution(mesh):
    in_specs = (
        P("rows", "freq"),
        P("rows", None),
        P("rows", None, None, None),
        P("freq", None),
        P(),
    )
    out_specs = P(None, ("rows", "freq"))
    return jax.shard_map(shards, mesh=mesh, in_specs=in_specs, out_specs=out_specs, check_vma=False)
```

```python
import jax
import jax.numpy as jnp
from jax import lax
from jax.sharding import PartitionSpec as P
from jax.experimental import pallas as pl
from jax.experimental.pallas import tpu as pltpu

HB = 2
POWER = 2


HIGHEST = lax.Precision.HIGHEST
HIGH = lax.Precision.HIGH


def extended_2(block, sides, width):
    for axis, dim in sides:
        count = lax.axis_size(axis)
        forward = [(i, i + 1) for i in range(count - 1)]
        backward = [(target, source) for source, target in forward]
        low = lax.ppermute(
            lax.slice_in_dim(block, block.shape[dim] - width, None, axis=dim), axis, forward
        )
        high = lax.ppermute(lax.slice_in_dim(block, 0, width, axis=dim), axis, backward)
        block = jnp.concatenate([low, block, high], axis=dim)
    return block


ROWS_PER_STEP = 16


def mass_kernel(index_ref, low_ref, own_ref, high_ref, mass_ref, out_ref, gram_ref):
    step = pl.program_id(0)
    size = mass_ref.shape[2]
    halo = low_ref.shape[0] // size
    own_tiles = own_ref.shape[0] // size
    rows_here = mass_ref.shape[0]
    kb = mass_ref.shape[1]

    @pl.when(step == 0)
    def _():
        gram_ref[...] = jnp.zeros(gram_ref.shape, gram_ref.dtype)

    for row in range(rows_here):
        block = step * rows_here + row
        total = jnp.zeros((size, out_ref.shape[1]), jnp.float32)
        for k in range(kb):
            tile_id = index_ref[block * kb + k]
            own_at = jnp.clip(tile_id - halo, 0, own_tiles - 1)
            low_at = jnp.clip(tile_id, 0, halo - 1)
            high_at = jnp.clip(tile_id - halo - own_tiles, 0, halo - 1)
            own_tile = own_ref[pl.ds(pl.multiple_of(own_at * size, size), size), :]
            low_tile = low_ref[pl.ds(pl.multiple_of(low_at * size, size), size), :]
            high_tile = high_ref[pl.ds(pl.multiple_of(high_at * size, size), size), :]
            tile = jnp.where(
                tile_id < halo, low_tile, jnp.where(tile_id >= halo + own_tiles, high_tile, own_tile)
            )
            total = total + jnp.dot(mass_ref[row, k], tile, preferred_element_type=jnp.float32)
        out_ref[row * size : (row + 1) * size, :] = total

    chunk = out_ref[...]
    high_part = chunk.astype(jnp.bfloat16)
    low_part = (chunk - high_part.astype(jnp.float32)).astype(jnp.bfloat16)
    dims = (((0,), (0,)), ((), ()))
    main = lax.dot_general(high_part, high_part, dims, preferred_element_type=jnp.float32)
    cross = lax.dot_general(high_part, low_part, dims, preferred_element_type=jnp.float32)
    gram_ref[...] += main + (cross + cross.T)


def apply_mass(low, own, high, mass_blocks, tile_index):
    blocks, kb, size, _ = mass_blocks.shape
    cols = own.shape[1]
    per = ROWS_PER_STEP
    grid_spec = pltpu.PrefetchScalarGridSpec(
        num_scalar_prefetch=1,
        grid=(blocks // per,),
        in_specs=[
            pl.BlockSpec(low.shape, lambda i, idx: (0, 0)),
            pl.BlockSpec(own.shape, lambda i, idx: (0, 0)),
            pl.BlockSpec(high.shape, lambda i, idx: (0, 0)),
            pl.BlockSpec((per, kb, size, size), lambda i, idx: (i, 0, 0, 0)),
        ],
        out_specs=[
            pl.BlockSpec((per * size, cols), lambda i, idx: (i, 0)),
            pl.BlockSpec((cols, cols), lambda i, idx: (0, 0)),
        ],
    )
    return pl.pallas_call(
        mass_kernel,
        grid_spec=grid_spec,
        out_shape=[
            jax.ShapeDtypeStruct((blocks * size, cols), jnp.float32),
            jax.ShapeDtypeStruct((cols, cols), jnp.float32),
        ],
        compiler_params=pltpu.CompilerParams(dimension_semantics=("arbitrary",)),
    )(tile_index.reshape(-1), low, own, high, mass_blocks)


def butterfly_sum(x, axes):
    for axis in axes:
        count = lax.axis_size(axis)
        step = 1
        while step < count:
            if step * 4 <= count:
                parts = [x]
                for mask in (1, 2, 3):
                    pairs = [
                        (i, (i & ~(3 * step)) | ((((i // step) & 3) ^ mask) * step))
                        for i in range(count)
                    ]
                    parts.append(lax.ppermute(x, axis, pairs))
                x = (parts[0] + parts[1]) + (parts[2] + parts[3])
                step *= 4
            else:
                x = x + lax.ppermute(x, axis, [(i, i ^ step) for i in range(count)])
                step *= 2
    return x


def orthonormal(columns_block):
    inner_gram = jnp.dot(columns_block.T, columns_block, precision=HIGHEST)
    lower_factor = jnp.linalg.cholesky(inner_gram)
    return lax.linalg.triangular_solve(
        lower_factor, columns_block, left_side=False, lower=True, transpose_a=True
    )


def subspace(gram_matrix, start_block):
    current = start_block
    for repeat in range(POWER):
        current = orthonormal(jnp.dot(gram_matrix, current, precision=HIGHEST))
    return current


def coefficient_tree(full_gram, start_merge, rank_size, freq_count):
    pairs = freq_count // 2
    width = 2 * rank_size
    blocks = jnp.stack(
        [full_gram[p * width : (p + 1) * width, p * width : (p + 1) * width] for p in range(pairs)]
    )
    pair_weights = jax.vmap(subspace, in_axes=(0, None))(blocks, start_merge)
    zero = jnp.zeros((width, rank_size), jnp.float32)
    coefficients = []
    for p in range(pairs):
        parts = [zero] * pairs
        parts[p] = pair_weights[p]
        coefficients.append(jnp.concatenate(parts, axis=0))
    while len(coefficients) > 1:
        merged = []
        for position in range(0, len(coefficients), 2):
            joined = jnp.concatenate([coefficients[position], coefficients[position + 1]], axis=1)
            pair_gram = jnp.dot(
                joined.T, jnp.dot(full_gram, joined, precision=HIGHEST), precision=HIGHEST
            )
            merged.append(jnp.dot(joined, subspace(pair_gram, start_merge), precision=HIGHEST))
        coefficients = merged
    return coefficients[0]


def shards(snapshots, block_cols, mass_blocks, start_group, start_merge):
    block_size = mass_blocks.shape[2]
    local_blocks = block_cols.shape[0]
    local_cols = snapshots.shape[1]
    total_rows = lax.axis_size("rows") * snapshots.shape[0]
    width = HB * block_size
    count = lax.axis_size("rows")
    forward = [(i, i + 1) for i in range(count - 1)]
    backward = [(target, source) for source, target in forward]
    low = lax.ppermute(snapshots[snapshots.shape[0] - width :], "rows", forward)
    high = lax.ppermute(snapshots[:width], "rows", backward)
    local_index = block_cols - lax.axis_index("rows") * local_blocks + HB
    weighted, local_gram = apply_mass(low, snapshots, high, mass_blocks, local_index)
    group_gram = butterfly_sum(local_gram, ("rows",)) / total_rows
    weights = subspace(group_gram, start_group)
    modes = lax.dot_general(weights, weighted, (((0,), (1,)), ((), ())), precision=HIGH)
    rank_size = modes.shape[0]
    freq_count = lax.axis_size("freq")
    group = lax.axis_index("freq")
    share = modes.shape[1] // freq_count
    received = [lax.dynamic_slice_in_dim(modes, group * share, share, 1)]
    for shift in range(1, freq_count):
        piece = lax.dynamic_slice_in_dim(modes, ((group + shift) % freq_count) * share, share, 1)
        pairs = [(i, (i + shift) % freq_count) for i in range(freq_count)]
        received.append(lax.ppermute(piece, "freq", pairs))
    stacked = jnp.concatenate(received, axis=0)
    source = (group - jnp.arange(freq_count)) % freq_count
    local_full = jnp.dot(stacked, stacked.T, precision=HIGH)
    blocked = local_full.reshape(freq_count, rank_size, freq_count, rank_size)
    blocked = jnp.take(jnp.take(blocked, source, axis=0), source, axis=2)
    full_gram = butterfly_sum(
        blocked.reshape(freq_count * rank_size, freq_count * rank_size), ("rows", "freq")
    ) / total_rows
    combined = coefficient_tree(full_gram, start_merge, rank_size, freq_count)
    shifted = jnp.take(combined.reshape(freq_count, rank_size, rank_size), source, axis=0)
    result = jnp.dot(shifted.reshape(freq_count * rank_size, rank_size).T, stacked, precision=HIGH)
    return result


def solution(mesh):
    in_specs = (
        P("rows", "freq"),
        P("rows", None),
        P("rows", None, None, None),
        P("freq", None),
        P(),
    )
    out_specs = P(None, ("rows", "freq"))
    return jax.shard_map(shards, mesh=mesh, in_specs=in_specs, out_specs=out_specs, check_vma=False)
```

```python
import jax
import jax.numpy as jnp
from jax import lax
from jax.sharding import PartitionSpec as P
from jax.experimental import pallas as pl
from jax.experimental.pallas import tpu as pltpu

HB = 2
POWER = 2


HIGHEST = lax.Precision.HIGHEST
HIGH = lax.Precision.HIGH


def extended_2(block, sides, width):
    for axis, dim in sides:
        count = lax.axis_size(axis)
        forward = [(i, i + 1) for i in range(count - 1)]
        backward = [(target, source) for source, target in forward]
        low = lax.ppermute(
            lax.slice_in_dim(block, block.shape[dim] - width, None, axis=dim), axis, forward
        )
        high = lax.ppermute(lax.slice_in_dim(block, 0, width, axis=dim), axis, backward)
        block = jnp.concatenate([low, block, high], axis=dim)
    return block


ROWS_PER_STEP = 16


def mass_kernel(index_ref, low_ref, own_ref, high_ref, mass_ref, out_ref, gram_ref):
    step = pl.program_id(0)
    size = mass_ref.shape[2]
    halo = low_ref.shape[0] // size
    own_tiles = own_ref.shape[0] // size
    rows_here = mass_ref.shape[0]
    kb = mass_ref.shape[1]

    @pl.when(step == 0)
    def _():
        gram_ref[...] = jnp.zeros(gram_ref.shape, gram_ref.dtype)

    for row in range(rows_here):
        block = step * rows_here + row
        total = jnp.zeros((size, out_ref.shape[1]), jnp.float32)
        for k in range(kb):
            tile_id = index_ref[block * kb + k]
            own_at = jnp.clip(tile_id - halo, 0, own_tiles - 1)
            low_at = jnp.clip(tile_id, 0, halo - 1)
            high_at = jnp.clip(tile_id - halo - own_tiles, 0, halo - 1)
            own_tile = own_ref[pl.ds(pl.multiple_of(own_at * size, size), size), :]
            low_tile = low_ref[pl.ds(pl.multiple_of(low_at * size, size), size), :]
            high_tile = high_ref[pl.ds(pl.multiple_of(high_at * size, size), size), :]
            tile = jnp.where(
                tile_id < halo, low_tile, jnp.where(tile_id >= halo + own_tiles, high_tile, own_tile)
            )
            total = total + jnp.dot(mass_ref[row, k], tile, preferred_element_type=jnp.float32)
        out_ref[row * size : (row + 1) * size, :] = total

    chunk = out_ref[...]
    high_part = chunk.astype(jnp.bfloat16)
    low_part = (chunk - high_part.astype(jnp.float32)).astype(jnp.bfloat16)
    dims = (((0,), (0,)), ((), ()))
    main = lax.dot_general(high_part, high_part, dims, preferred_element_type=jnp.float32)
    cross = lax.dot_general(high_part, low_part, dims, preferred_element_type=jnp.float32)
    gram_ref[...] += main + (cross + cross.T)


def apply_mass(low, own, high, mass_blocks, tile_index):
    blocks, kb, size, _ = mass_blocks.shape
    cols = own.shape[1]
    per = ROWS_PER_STEP
    grid_spec = pltpu.PrefetchScalarGridSpec(
        num_scalar_prefetch=1,
        grid=(blocks // per,),
        in_specs=[
            pl.BlockSpec(low.shape, lambda i, idx: (0, 0)),
            pl.BlockSpec(own.shape, lambda i, idx: (0, 0)),
            pl.BlockSpec(high.shape, lambda i, idx: (0, 0)),
            pl.BlockSpec((per, kb, size, size), lambda i, idx: (i, 0, 0, 0)),
        ],
        out_specs=[
            pl.BlockSpec((per * size, cols), lambda i, idx: (i, 0)),
            pl.BlockSpec((cols, cols), lambda i, idx: (0, 0)),
        ],
    )
    return pl.pallas_call(
        mass_kernel,
        grid_spec=grid_spec,
        out_shape=[
            jax.ShapeDtypeStruct((blocks * size, cols), jnp.float32),
            jax.ShapeDtypeStruct((cols, cols), jnp.float32),
        ],
        compiler_params=pltpu.CompilerParams(dimension_semantics=("arbitrary",)),
    )(tile_index.reshape(-1), low, own, high, mass_blocks)


def butterfly_sum(x, axes):
    for axis in axes:
        count = lax.axis_size(axis)
        step = 1
        while step < count:
            if step * 4 <= count:
                parts = [x]
                for mask in (1, 2, 3):
                    pairs = [
                        (i, (i & ~(3 * step)) | ((((i // step) & 3) ^ mask) * step))
                        for i in range(count)
                    ]
                    parts.append(lax.ppermute(x, axis, pairs))
                x = (parts[0] + parts[1]) + (parts[2] + parts[3])
                step *= 4
            else:
                x = x + lax.ppermute(x, axis, [(i, i ^ step) for i in range(count)])
                step *= 2
    return x


def subspace_kernel(g_ref, v_ref, out_ref):
    gram = g_ref[...]
    current = v_ref[...]
    rank = current.shape[0]
    nt = (((1,), (1,)), ((), ()))
    sub = lax.broadcasted_iota(jnp.int32, (rank, rank), 0)
    lane = lax.broadcasted_iota(jnp.int32, (rank, rank), 1)
    sub_wide = lax.broadcasted_iota(jnp.int32, current.shape, 0)
    for repeat in range(POWER):
        product = lax.dot_general(current, gram, nt, precision=HIGHEST, preferred_element_type=jnp.float32)
        inner = lax.dot_general(product, product, nt, precision=HIGHEST, preferred_element_type=jnp.float32)

        def one_column(j, carry):
            inner, rest, solved = carry
            row = jnp.sum(jnp.where(sub == j, inner, 0.0), axis=0, keepdims=True)
            col = jnp.sum(jnp.where(lane == j, inner, 0.0), axis=1, keepdims=True)
            pivot = jnp.sum(jnp.where(lane[:1] == j, row, 0.0), axis=1, keepdims=True)
            root = jnp.sqrt(pivot)
            factor_row = jnp.where(lane[:1] >= j, row / root, 0.0)
            factor_col = jnp.where(sub[:, :1] >= j, col / root, 0.0)
            inner = inner - factor_col * factor_row
            answer = jnp.sum(jnp.where(sub_wide == j, rest, 0.0), axis=0, keepdims=True) / root
            rest = rest - factor_row.T * answer
            solved = jnp.where(sub_wide == j, answer, solved)
            return inner, rest, solved

        _, _, current = lax.fori_loop(
            0, rank, one_column, (inner, product, jnp.zeros_like(product)), unroll=True
        )
    out_ref[...] = current


def subspace_batch(grams, starts_t):
    batch, size, _ = grams.shape
    rank = starts_t.shape[1]
    return pl.pallas_call(
        subspace_kernel,
        grid=(batch,),
        in_specs=[
            pl.BlockSpec((None, size, size), lambda b: (b, 0, 0)),
            pl.BlockSpec((None, rank, size), lambda b: (b, 0, 0)),
        ],
        out_specs=pl.BlockSpec((None, rank, size), lambda b: (b, 0, 0)),
        out_shape=jax.ShapeDtypeStruct((batch, rank, size), jnp.float32),
    )(grams, starts_t)


def fast_subspace(gram_matrix, start_block):
    return subspace_batch(gram_matrix[None], start_block.T[None])[0].T


def orthonormal(columns_block):
    inner_gram = jnp.dot(columns_block.T, columns_block, precision=HIGHEST)
    lower_factor = jnp.linalg.cholesky(inner_gram)
    return lax.linalg.triangular_solve(
        lower_factor, columns_block, left_side=False, lower=True, transpose_a=True
    )


def subspace(gram_matrix, start_block):
    current = start_block
    for repeat in range(POWER):
        current = orthonormal(jnp.dot(gram_matrix, current, precision=HIGHEST))
    return current


def coefficient_tree(full_gram, start_merge, rank_size, freq_count):
    pairs = freq_count // 2
    width = 2 * rank_size
    blocks = jnp.stack(
        [full_gram[p * width : (p + 1) * width, p * width : (p + 1) * width] for p in range(pairs)]
    )
    starts_t = jnp.broadcast_to(start_merge.T[None], (pairs,) + start_merge.T.shape)
    pair_weights = jnp.swapaxes(subspace_batch(blocks, starts_t), 1, 2)
    zero = jnp.zeros((width, rank_size), jnp.float32)
    coefficients = []
    for p in range(pairs):
        parts = [zero] * pairs
        parts[p] = pair_weights[p]
        coefficients.append(jnp.concatenate(parts, axis=0))
    while len(coefficients) > 1:
        merged = []
        for position in range(0, len(coefficients), 2):
            joined = jnp.concatenate([coefficients[position], coefficients[position + 1]], axis=1)
            pair_gram = jnp.dot(
                joined.T, jnp.dot(full_gram, joined, precision=HIGHEST), precision=HIGHEST
            )
            merged.append(jnp.dot(joined, fast_subspace(pair_gram, start_merge), precision=HIGHEST))
        coefficients = merged
    return coefficients[0]


def shards(snapshots, block_cols, mass_blocks, start_group, start_merge):
    block_size = mass_blocks.shape[2]
    local_blocks = block_cols.shape[0]
    local_cols = snapshots.shape[1]
    total_rows = lax.axis_size("rows") * snapshots.shape[0]
    width = HB * block_size
    count = lax.axis_size("rows")
    forward = [(i, i + 1) for i in range(count - 1)]
    backward = [(target, source) for source, target in forward]
    low = lax.ppermute(snapshots[snapshots.shape[0] - width :], "rows", forward)
    high = lax.ppermute(snapshots[:width], "rows", backward)
    local_index = block_cols - lax.axis_index("rows") * local_blocks + HB
    weighted, local_gram = apply_mass(low, snapshots, high, mass_blocks, local_index)
    group_gram = butterfly_sum(local_gram, ("rows",)) / total_rows
    weights = fast_subspace(group_gram, start_group)
    modes = lax.dot_general(weights, weighted, (((0,), (1,)), ((), ())), precision=HIGH)
    rank_size = modes.shape[0]
    freq_count = lax.axis_size("freq")
    group = lax.axis_index("freq")
    share = modes.shape[1] // freq_count
    received = [lax.dynamic_slice_in_dim(modes, group * share, share, 1)]
    for shift in range(1, freq_count):
        piece = lax.dynamic_slice_in_dim(modes, ((group + shift) % freq_count) * share, share, 1)
        pairs = [(i, (i + shift) % freq_count) for i in range(freq_count)]
        received.append(lax.ppermute(piece, "freq", pairs))
    stacked = jnp.concatenate(received, axis=0)
    source = (group - jnp.arange(freq_count)) % freq_count
    local_full = jnp.dot(stacked, stacked.T, precision=HIGH)
    blocked = local_full.reshape(freq_count, rank_size, freq_count, rank_size)
    blocked = jnp.take(jnp.take(blocked, source, axis=0), source, axis=2)
    full_gram = butterfly_sum(
        blocked.reshape(freq_count * rank_size, freq_count * rank_size), ("rows", "freq")
    ) / total_rows
    combined = coefficient_tree(full_gram, start_merge, rank_size, freq_count)
    shifted = jnp.take(combined.reshape(freq_count, rank_size, rank_size), source, axis=0)
    result = jnp.dot(shifted.reshape(freq_count * rank_size, rank_size).T, stacked, precision=HIGH)
    return result


def solution(mesh):
    in_specs = (
        P("rows", "freq"),
        P("rows", None),
        P("rows", None, None, None),
        P("freq", None),
        P(),
    )
    out_specs = P(None, ("rows", "freq"))
    return jax.shard_map(shards, mesh=mesh, in_specs=in_specs, out_specs=out_specs, check_vma=False)
```

```python
import jax
import jax.numpy as jnp
from jax import lax
from jax.sharding import PartitionSpec as P
from jax.experimental import pallas as pl
from jax.experimental.pallas import tpu as pltpu

HB = 2
POWER = 2


HIGHEST = lax.Precision.HIGHEST
HIGH = lax.Precision.HIGH


def extended_2(block, sides, width):
    for axis, dim in sides:
        count = lax.axis_size(axis)
        forward = [(i, i + 1) for i in range(count - 1)]
        backward = [(target, source) for source, target in forward]
        low = lax.ppermute(
            lax.slice_in_dim(block, block.shape[dim] - width, None, axis=dim), axis, forward
        )
        high = lax.ppermute(lax.slice_in_dim(block, 0, width, axis=dim), axis, backward)
        block = jnp.concatenate([low, block, high], axis=dim)
    return block


ROWS_PER_STEP = 16


def mass_kernel(index_ref, low_ref, own_ref, high_ref, mass_ref, out_ref, gram_ref):
    step = pl.program_id(0)
    size = mass_ref.shape[2]
    halo = low_ref.shape[0] // size
    own_tiles = own_ref.shape[0] // size
    rows_here = mass_ref.shape[0]
    kb = mass_ref.shape[1]

    @pl.when(step == 0)
    def _():
        gram_ref[...] = jnp.zeros(gram_ref.shape, gram_ref.dtype)

    for row in range(rows_here):
        block = step * rows_here + row
        total = jnp.zeros((size, out_ref.shape[1]), jnp.float32)
        for k in range(kb):
            tile_id = index_ref[block * kb + k]
            own_at = jnp.clip(tile_id - halo, 0, own_tiles - 1)
            low_at = jnp.clip(tile_id, 0, halo - 1)
            high_at = jnp.clip(tile_id - halo - own_tiles, 0, halo - 1)
            own_tile = own_ref[pl.ds(pl.multiple_of(own_at * size, size), size), :]
            low_tile = low_ref[pl.ds(pl.multiple_of(low_at * size, size), size), :]
            high_tile = high_ref[pl.ds(pl.multiple_of(high_at * size, size), size), :]
            tile = jnp.where(
                tile_id < halo, low_tile, jnp.where(tile_id >= halo + own_tiles, high_tile, own_tile)
            )
            total = total + jnp.dot(mass_ref[row, k], tile, preferred_element_type=jnp.float32)
        out_ref[row * size : (row + 1) * size, :] = total

    chunk = out_ref[...]
    high_part = chunk.astype(jnp.bfloat16)
    low_part = (chunk - high_part.astype(jnp.float32)).astype(jnp.bfloat16)
    dims = (((0,), (0,)), ((), ()))
    main = lax.dot_general(high_part, high_part, dims, preferred_element_type=jnp.float32)
    cross = lax.dot_general(high_part, low_part, dims, preferred_element_type=jnp.float32)
    gram_ref[...] += main + (cross + cross.T)


def apply_mass(low, own, high, mass_blocks, tile_index):
    blocks, kb, size, _ = mass_blocks.shape
    cols = own.shape[1]
    per = ROWS_PER_STEP
    grid_spec = pltpu.PrefetchScalarGridSpec(
        num_scalar_prefetch=1,
        grid=(blocks // per,),
        in_specs=[
            pl.BlockSpec(low.shape, lambda i, idx: (0, 0)),
            pl.BlockSpec(own.shape, lambda i, idx: (0, 0)),
            pl.BlockSpec(high.shape, lambda i, idx: (0, 0)),
            pl.BlockSpec((per, kb, size, size), lambda i, idx: (i, 0, 0, 0)),
        ],
        out_specs=[
            pl.BlockSpec((per * size, cols), lambda i, idx: (i, 0)),
            pl.BlockSpec((cols, cols), lambda i, idx: (0, 0)),
        ],
    )
    return pl.pallas_call(
        mass_kernel,
        grid_spec=grid_spec,
        out_shape=[
            jax.ShapeDtypeStruct((blocks * size, cols), jnp.float32),
            jax.ShapeDtypeStruct((cols, cols), jnp.float32),
        ],
        compiler_params=pltpu.CompilerParams(dimension_semantics=("arbitrary",)),
    )(tile_index.reshape(-1), low, own, high, mass_blocks)


def butterfly_sum(x, axes):
    for axis in axes:
        count = lax.axis_size(axis)
        step = 1
        while step < count:
            if step * 4 <= count:
                parts = [x]
                for mask in (1, 2, 3):
                    pairs = [
                        (i, (i & ~(3 * step)) | ((((i // step) & 3) ^ mask) * step))
                        for i in range(count)
                    ]
                    parts.append(lax.ppermute(x, axis, pairs))
                x = (parts[0] + parts[1]) + (parts[2] + parts[3])
                step *= 4
            else:
                x = x + lax.ppermute(x, axis, [(i, i ^ step) for i in range(count)])
                step *= 2
    return x


def subspace_kernel(g_ref, v_ref, out_ref):
    batch = g_ref.shape[0]
    rank = v_ref.shape[1]
    nt = (((1,), (1,)), ((), ()))
    sub = lax.broadcasted_iota(jnp.int32, (rank, rank), 0)
    lane = lax.broadcasted_iota(jnp.int32, (rank, rank), 1)
    sub_wide = lax.broadcasted_iota(jnp.int32, v_ref.shape[1:], 0)
    grams = [g_ref[b] for b in range(batch)]
    currents = [v_ref[b] for b in range(batch)]
    for repeat in range(POWER):
        carry = []
        for b in range(batch):
            product = lax.dot_general(
                currents[b], grams[b], nt, precision=HIGHEST, preferred_element_type=jnp.float32
            )
            inner = lax.dot_general(product, product, nt, precision=HIGHEST, preferred_element_type=jnp.float32)
            carry.append((inner, product, jnp.zeros_like(product)))

        def one_column(j, carry):
            out = []
            for inner, rest, solved in carry:
                row = jnp.sum(jnp.where(sub == j, inner, 0.0), axis=0, keepdims=True)
                col = jnp.sum(jnp.where(lane == j, inner, 0.0), axis=1, keepdims=True)
                pivot = jnp.sum(jnp.where(lane[:1] == j, row, 0.0), axis=1, keepdims=True)
                root = jnp.sqrt(pivot)
                factor_row = jnp.where(lane[:1] >= j, row / root, 0.0)
                factor_col = jnp.where(sub[:, :1] >= j, col / root, 0.0)
                inner = inner - factor_col * factor_row
                answer = jnp.sum(jnp.where(sub_wide == j, rest, 0.0), axis=0, keepdims=True) / root
                rest = rest - factor_col * answer
                solved = jnp.where(sub_wide == j, answer, solved)
                out.append((inner, rest, solved))
            return tuple(out)

        carry = lax.fori_loop(0, rank, one_column, tuple(carry), unroll=True)
        currents = [solved for _, _, solved in carry]
    for b in range(batch):
        out_ref[b] = currents[b]


def subspace_batch(grams, starts_t):
    batch, size, _ = grams.shape
    rank = starts_t.shape[1]
    return pl.pallas_call(
        subspace_kernel,
        out_shape=jax.ShapeDtypeStruct((batch, rank, size), jnp.float32),
    )(grams, starts_t)


def fast_subspace(gram_matrix, start_block):
    return subspace_batch(gram_matrix[None], start_block.T[None])[0].T


def orthonormal(columns_block):
    inner_gram = jnp.dot(columns_block.T, columns_block, precision=HIGHEST)
    lower_factor = jnp.linalg.cholesky(inner_gram)
    return lax.linalg.triangular_solve(
        lower_factor, columns_block, left_side=False, lower=True, transpose_a=True
    )


def subspace(gram_matrix, start_block):
    current = start_block
    for repeat in range(POWER):
        current = orthonormal(jnp.dot(gram_matrix, current, precision=HIGHEST))
    return current


def coefficient_tree(full_gram, start_merge, rank_size, freq_count):
    pairs = freq_count // 2
    width = 2 * rank_size
    blocks = jnp.stack(
        [full_gram[p * width : (p + 1) * width, p * width : (p + 1) * width] for p in range(pairs)]
    )
    starts_t = jnp.broadcast_to(start_merge.T[None], (pairs,) + start_merge.T.shape)
    pair_weights = jnp.swapaxes(subspace_batch(blocks, starts_t), 1, 2)
    zero = jnp.zeros((width, rank_size), jnp.float32)
    coefficients = []
    for p in range(pairs):
        parts = [zero] * pairs
        parts[p] = pair_weights[p]
        coefficients.append(jnp.concatenate(parts, axis=0))
    while len(coefficients) > 1:
        merged = []
        for position in range(0, len(coefficients), 2):
            joined = jnp.concatenate([coefficients[position], coefficients[position + 1]], axis=1)
            pair_gram = jnp.dot(
                joined.T, jnp.dot(full_gram, joined, precision=HIGHEST), precision=HIGHEST
            )
            merged.append(jnp.dot(joined, fast_subspace(pair_gram, start_merge), precision=HIGHEST))
        coefficients = merged
    return coefficients[0]


def shards(snapshots, block_cols, mass_blocks, start_group, start_merge):
    block_size = mass_blocks.shape[2]
    local_blocks = block_cols.shape[0]
    local_cols = snapshots.shape[1]
    total_rows = lax.axis_size("rows") * snapshots.shape[0]
    width = HB * block_size
    count = lax.axis_size("rows")
    forward = [(i, i + 1) for i in range(count - 1)]
    backward = [(target, source) for source, target in forward]
    low = lax.ppermute(snapshots[snapshots.shape[0] - width :], "rows", forward)
    high = lax.ppermute(snapshots[:width], "rows", backward)
    local_index = block_cols - lax.axis_index("rows") * local_blocks + HB
    weighted, local_gram = apply_mass(low, snapshots, high, mass_blocks, local_index)
    group_gram = butterfly_sum(local_gram, ("rows",)) / total_rows
    weights = fast_subspace(group_gram, start_group)
    rank_size = weights.shape[1]
    freq_count = lax.axis_size("freq")
    group = lax.axis_index("freq")
    share = weighted.shape[0] // freq_count

    def modes_of(part):
        rows_part = lax.dynamic_slice_in_dim(weighted, part * share, share, 0)
        return lax.dot_general(weights, rows_part, (((0,), (1,)), ((), ())), precision=HIGH)

    received = [None] * freq_count
    for shift in range(1, freq_count):
        piece = modes_of((group + shift) % freq_count)
        pairs = [(i, (i + shift) % freq_count) for i in range(freq_count)]
        received[shift] = lax.ppermute(piece, "freq", pairs)
    received[0] = modes_of(group)
    stacked = jnp.concatenate(received, axis=0)
    source = (group - jnp.arange(freq_count)) % freq_count
    local_full = jnp.dot(stacked, stacked.T, precision=HIGH)
    blocked = local_full.reshape(freq_count, rank_size, freq_count, rank_size)
    blocked = jnp.take(jnp.take(blocked, source, axis=0), source, axis=2)
    full_gram = butterfly_sum(
        blocked.reshape(freq_count * rank_size, freq_count * rank_size), ("rows", "freq")
    ) / total_rows
    combined = coefficient_tree(full_gram, start_merge, rank_size, freq_count)
    shifted = jnp.take(combined.reshape(freq_count, rank_size, rank_size), source, axis=0)
    result = jnp.dot(shifted.reshape(freq_count * rank_size, rank_size).T, stacked, precision=HIGH)
    return result


def solution(mesh):
    in_specs = (
        P("rows", "freq"),
        P("rows", None),
        P("rows", None, None, None),
        P("freq", None),
        P(),
    )
    out_specs = P(None, ("rows", "freq"))
    return jax.shard_map(shards, mesh=mesh, in_specs=in_specs, out_specs=out_specs, check_vma=False)
```

```python
import jax
import jax.numpy as jnp
from jax import lax
from jax.sharding import PartitionSpec as P
from jax.experimental import pallas as pl
from jax.experimental.pallas import tpu as pltpu

HB = 2
POWER = 2


HIGHEST = lax.Precision.HIGHEST
HIGH = lax.Precision.HIGH


def extended_2(block, sides, width):
    for axis, dim in sides:
        count = lax.axis_size(axis)
        forward = [(i, i + 1) for i in range(count - 1)]
        backward = [(target, source) for source, target in forward]
        low = lax.ppermute(
            lax.slice_in_dim(block, block.shape[dim] - width, None, axis=dim), axis, forward
        )
        high = lax.ppermute(lax.slice_in_dim(block, 0, width, axis=dim), axis, backward)
        block = jnp.concatenate([low, block, high], axis=dim)
    return block


ROWS_PER_STEP = 16


def mass_kernel(index_ref, low_ref, own_ref, high_ref, mass_ref, out_ref, gram_ref):
    step = pl.program_id(0)
    size = mass_ref.shape[2]
    halo = low_ref.shape[0] // size
    own_tiles = own_ref.shape[0] // size
    rows_here = mass_ref.shape[0]
    kb = mass_ref.shape[1]

    @pl.when(step == 0)
    def _():
        gram_ref[...] = jnp.zeros(gram_ref.shape, gram_ref.dtype)

    for row in range(rows_here):
        block = step * rows_here + row
        total = jnp.zeros((size, out_ref.shape[1]), jnp.float32)
        for k in range(kb):
            tile_id = index_ref[block * kb + k]
            own_at = jnp.clip(tile_id - halo, 0, own_tiles - 1)
            low_at = jnp.clip(tile_id, 0, halo - 1)
            high_at = jnp.clip(tile_id - halo - own_tiles, 0, halo - 1)
            own_tile = own_ref[pl.ds(pl.multiple_of(own_at * size, size), size), :]
            low_tile = low_ref[pl.ds(pl.multiple_of(low_at * size, size), size), :]
            high_tile = high_ref[pl.ds(pl.multiple_of(high_at * size, size), size), :]
            tile = jnp.where(
                tile_id < halo, low_tile, jnp.where(tile_id >= halo + own_tiles, high_tile, own_tile)
            )
            total = total + jnp.dot(mass_ref[row, k], tile, preferred_element_type=jnp.float32)
        out_ref[row * size : (row + 1) * size, :] = total

    chunk = out_ref[...]
    high_part = chunk.astype(jnp.bfloat16)
    low_part = (chunk - high_part.astype(jnp.float32)).astype(jnp.bfloat16)
    dims = (((0,), (0,)), ((), ()))
    main = lax.dot_general(high_part, high_part, dims, preferred_element_type=jnp.float32)
    cross = lax.dot_general(high_part, low_part, dims, preferred_element_type=jnp.float32)
    gram_ref[...] += main + (cross + cross.T)


def apply_mass(low, own, high, mass_blocks, tile_index):
    blocks, kb, size, _ = mass_blocks.shape
    cols = own.shape[1]
    per = ROWS_PER_STEP
    grid_spec = pltpu.PrefetchScalarGridSpec(
        num_scalar_prefetch=1,
        grid=(blocks // per,),
        in_specs=[
            pl.BlockSpec(low.shape, lambda i, idx: (0, 0)),
            pl.BlockSpec(own.shape, lambda i, idx: (0, 0)),
            pl.BlockSpec(high.shape, lambda i, idx: (0, 0)),
            pl.BlockSpec((per, kb, size, size), lambda i, idx: (i, 0, 0, 0)),
        ],
        out_specs=[
            pl.BlockSpec((per * size, cols), lambda i, idx: (i, 0)),
            pl.BlockSpec((cols, cols), lambda i, idx: (0, 0)),
        ],
    )
    return pl.pallas_call(
        mass_kernel,
        grid_spec=grid_spec,
        out_shape=[
            jax.ShapeDtypeStruct((blocks * size, cols), jnp.float32),
            jax.ShapeDtypeStruct((cols, cols), jnp.float32),
        ],
        compiler_params=pltpu.CompilerParams(dimension_semantics=("arbitrary",)),
    )(tile_index.reshape(-1), low, own, high, mass_blocks)


def butterfly_sum(x, axes):
    for axis in axes:
        count = lax.axis_size(axis)
        step = 1
        while step < count:
            if step * 4 <= count:
                parts = [x]
                for mask in (1, 2, 3):
                    pairs = [
                        (i, (i & ~(3 * step)) | ((((i // step) & 3) ^ mask) * step))
                        for i in range(count)
                    ]
                    parts.append(lax.ppermute(x, axis, pairs))
                x = (parts[0] + parts[1]) + (parts[2] + parts[3])
                step *= 4
            else:
                x = x + lax.ppermute(x, axis, [(i, i ^ step) for i in range(count)])
                step *= 2
    return x


def subspace_kernel(g_ref, v_ref, out_ref):
    batch = g_ref.shape[0]
    rank = v_ref.shape[1]
    nt = (((1,), (1,)), ((), ()))
    sub = lax.broadcasted_iota(jnp.int32, (rank, rank), 0)
    lane = lax.broadcasted_iota(jnp.int32, (rank, rank), 1)
    sub_wide = lax.broadcasted_iota(jnp.int32, v_ref.shape[1:], 0)
    grams = [g_ref[b] for b in range(batch)]
    currents = [v_ref[b] for b in range(batch)]
    for repeat in range(POWER):
        carry = []
        for b in range(batch):
            product = lax.dot_general(
                currents[b], grams[b], nt, precision=HIGHEST, preferred_element_type=jnp.float32
            )
            inner = lax.dot_general(product, product, nt, precision=HIGHEST, preferred_element_type=jnp.float32)
            carry.append((inner, product, jnp.zeros_like(product)))

        def one_column(j, carry):
            out = []
            for inner, rest, solved in carry:
                row = jnp.sum(jnp.where(sub == j, inner, 0.0), axis=0, keepdims=True)
                col = jnp.sum(jnp.where(lane == j, inner, 0.0), axis=1, keepdims=True)
                pivot = jnp.sum(jnp.where(lane[:1] == j, row, 0.0), axis=1, keepdims=True)
                scale = lax.rsqrt(pivot)
                factor_row = jnp.where(lane[:1] >= j, row * scale, 0.0)
                factor_col = jnp.where(sub[:, :1] >= j, col * scale, 0.0)
                inner = inner - factor_col * factor_row
                answer = jnp.sum(jnp.where(sub_wide == j, rest, 0.0), axis=0, keepdims=True) * scale
                rest = rest - factor_col * answer
                solved = jnp.where(sub_wide == j, answer, solved)
                out.append((inner, rest, solved))
            return tuple(out)

        carry = lax.fori_loop(0, rank, one_column, tuple(carry), unroll=True)
        currents = [solved for _, _, solved in carry]
    for b in range(batch):
        out_ref[b] = currents[b]


def subspace_batch(grams, starts_t):
    batch, size, _ = grams.shape
    rank = starts_t.shape[1]
    return pl.pallas_call(
        subspace_kernel,
        out_shape=jax.ShapeDtypeStruct((batch, rank, size), jnp.float32),
    )(grams, starts_t)


def fast_subspace(gram_matrix, start_block):
    return subspace_batch(gram_matrix[None], start_block.T[None])[0].T


def orthonormal(columns_block):
    inner_gram = jnp.dot(columns_block.T, columns_block, precision=HIGHEST)
    lower_factor = jnp.linalg.cholesky(inner_gram)
    return lax.linalg.triangular_solve(
        lower_factor, columns_block, left_side=False, lower=True, transpose_a=True
    )


def subspace(gram_matrix, start_block):
    current = start_block
    for repeat in range(POWER):
        current = orthonormal(jnp.dot(gram_matrix, current, precision=HIGHEST))
    return current


def coefficient_tree(full_gram, start_merge, rank_size, freq_count):
    pairs = freq_count // 2
    width = 2 * rank_size
    blocks = jnp.stack(
        [full_gram[p * width : (p + 1) * width, p * width : (p + 1) * width] for p in range(pairs)]
    )
    starts_t = jnp.broadcast_to(start_merge.T[None], (pairs,) + start_merge.T.shape)
    pair_weights = jnp.swapaxes(subspace_batch(blocks, starts_t), 1, 2)
    zero = jnp.zeros((width, rank_size), jnp.float32)
    coefficients = []
    for p in range(pairs):
        parts = [zero] * pairs
        parts[p] = pair_weights[p]
        coefficients.append(jnp.concatenate(parts, axis=0))
    while len(coefficients) > 1:
        merged = []
        for position in range(0, len(coefficients), 2):
            joined = jnp.concatenate([coefficients[position], coefficients[position + 1]], axis=1)
            pair_gram = jnp.dot(
                joined.T, jnp.dot(full_gram, joined, precision=HIGHEST), precision=HIGHEST
            )
            merged.append(jnp.dot(joined, fast_subspace(pair_gram, start_merge), precision=HIGHEST))
        coefficients = merged
    return coefficients[0]


def shards(snapshots, block_cols, mass_blocks, start_group, start_merge):
    block_size = mass_blocks.shape[2]
    local_blocks = block_cols.shape[0]
    local_cols = snapshots.shape[1]
    total_rows = lax.axis_size("rows") * snapshots.shape[0]
    width = HB * block_size
    count = lax.axis_size("rows")
    forward = [(i, i + 1) for i in range(count - 1)]
    backward = [(target, source) for source, target in forward]
    low = lax.ppermute(snapshots[snapshots.shape[0] - width :], "rows", forward)
    high = lax.ppermute(snapshots[:width], "rows", backward)
    local_index = block_cols - lax.axis_index("rows") * local_blocks + HB
    weighted, local_gram = apply_mass(low, snapshots, high, mass_blocks, local_index)
    group_gram = butterfly_sum(local_gram, ("rows",)) / total_rows
    weights = fast_subspace(group_gram, start_group)
    rank_size = weights.shape[1]
    freq_count = lax.axis_size("freq")
    group = lax.axis_index("freq")
    share = weighted.shape[0] // freq_count

    def modes_of(part):
        rows_part = lax.dynamic_slice_in_dim(weighted, part * share, share, 0)
        return lax.dot_general(weights, rows_part, (((0,), (1,)), ((), ())), precision=HIGH)

    received = [None] * freq_count
    for shift in range(1, freq_count):
        piece = modes_of((group + shift) % freq_count)
        pairs = [(i, (i + shift) % freq_count) for i in range(freq_count)]
        received[shift] = lax.ppermute(piece, "freq", pairs)
    received[0] = modes_of(group)
    stacked = jnp.concatenate(received, axis=0)
    source = (group - jnp.arange(freq_count)) % freq_count
    local_full = jnp.dot(stacked, stacked.T, precision=HIGH)
    blocked = local_full.reshape(freq_count, rank_size, freq_count, rank_size)
    blocked = jnp.take(jnp.take(blocked, source, axis=0), source, axis=2)
    full_gram = butterfly_sum(
        blocked.reshape(freq_count * rank_size, freq_count * rank_size), ("rows", "freq")
    ) / total_rows
    combined = coefficient_tree(full_gram, start_merge, rank_size, freq_count)
    shifted = jnp.take(combined.reshape(freq_count, rank_size, rank_size), source, axis=0)
    result = jnp.dot(shifted.reshape(freq_count * rank_size, rank_size).T, stacked, precision=HIGH)
    return result


def solution(mesh):
    in_specs = (
        P("rows", "freq"),
        P("rows", None),
        P("rows", None, None, None),
        P("freq", None),
        P(),
    )
    out_specs = P(None, ("rows", "freq"))
    return jax.shard_map(shards, mesh=mesh, in_specs=in_specs, out_specs=out_specs, check_vma=False)
```

```python
import jax
import jax.numpy as jnp
from jax import lax
from jax.sharding import PartitionSpec as P
from jax.experimental import pallas as pl
from jax.experimental.pallas import tpu as pltpu

HB = 2
POWER = 2


HIGHEST = lax.Precision.HIGHEST
HIGH = lax.Precision.HIGH


def extended_2(block, sides, width):
    for axis, dim in sides:
        count = lax.axis_size(axis)
        forward = [(i, i + 1) for i in range(count - 1)]
        backward = [(target, source) for source, target in forward]
        low = lax.ppermute(
            lax.slice_in_dim(block, block.shape[dim] - width, None, axis=dim), axis, forward
        )
        high = lax.ppermute(lax.slice_in_dim(block, 0, width, axis=dim), axis, backward)
        block = jnp.concatenate([low, block, high], axis=dim)
    return block


ROWS_PER_STEP = 16


def mass_kernel(index_ref, low_ref, own_ref, high_ref, mass_ref, out_ref, gram_ref):
    step = pl.program_id(0)
    size = mass_ref.shape[2]
    halo = low_ref.shape[0] // size
    own_tiles = own_ref.shape[0] // size
    rows_here = mass_ref.shape[0]
    kb = mass_ref.shape[1]

    @pl.when(step == 0)
    def _():
        gram_ref[...] = jnp.zeros(gram_ref.shape, gram_ref.dtype)

    for row in range(rows_here):
        block = step * rows_here + row
        total = jnp.zeros((size, out_ref.shape[1]), jnp.float32)
        for k in range(kb):
            tile_id = index_ref[block * kb + k]
            own_at = jnp.clip(tile_id - halo, 0, own_tiles - 1)
            low_at = jnp.clip(tile_id, 0, halo - 1)
            high_at = jnp.clip(tile_id - halo - own_tiles, 0, halo - 1)
            own_tile = own_ref[pl.ds(pl.multiple_of(own_at * size, size), size), :]
            low_tile = low_ref[pl.ds(pl.multiple_of(low_at * size, size), size), :]
            high_tile = high_ref[pl.ds(pl.multiple_of(high_at * size, size), size), :]
            tile = jnp.where(
                tile_id < halo, low_tile, jnp.where(tile_id >= halo + own_tiles, high_tile, own_tile)
            )
            total = total + jnp.dot(mass_ref[row, k], tile, preferred_element_type=jnp.float32)
        out_ref[row * size : (row + 1) * size, :] = total

    chunk = out_ref[...]
    high_part = chunk.astype(jnp.bfloat16)
    low_part = (chunk - high_part.astype(jnp.float32)).astype(jnp.bfloat16)
    dims = (((0,), (0,)), ((), ()))
    main = lax.dot_general(high_part, high_part, dims, preferred_element_type=jnp.float32)
    cross = lax.dot_general(high_part, low_part, dims, preferred_element_type=jnp.float32)
    gram_ref[...] += main + (cross + cross.T)


def apply_mass(low, own, high, mass_blocks, tile_index):
    blocks, kb, size, _ = mass_blocks.shape
    cols = own.shape[1]
    per = ROWS_PER_STEP
    grid_spec = pltpu.PrefetchScalarGridSpec(
        num_scalar_prefetch=1,
        grid=(blocks // per,),
        in_specs=[
            pl.BlockSpec(low.shape, lambda i, idx: (0, 0)),
            pl.BlockSpec(own.shape, lambda i, idx: (0, 0)),
            pl.BlockSpec(high.shape, lambda i, idx: (0, 0)),
            pl.BlockSpec((per, kb, size, size), lambda i, idx: (i, 0, 0, 0)),
        ],
        out_specs=[
            pl.BlockSpec((per * size, cols), lambda i, idx: (i, 0)),
            pl.BlockSpec((cols, cols), lambda i, idx: (0, 0)),
        ],
    )
    return pl.pallas_call(
        mass_kernel,
        grid_spec=grid_spec,
        out_shape=[
            jax.ShapeDtypeStruct((blocks * size, cols), jnp.float32),
            jax.ShapeDtypeStruct((cols, cols), jnp.float32),
        ],
        compiler_params=pltpu.CompilerParams(dimension_semantics=("arbitrary",)),
    )(tile_index.reshape(-1), low, own, high, mass_blocks)


def butterfly_sum(x, axes):
    for axis in axes:
        count = lax.axis_size(axis)
        step = 1
        while step < count:
            if step * 4 <= count:
                parts = [x]
                for mask in (1, 2, 3):
                    pairs = [
                        (i, (i & ~(3 * step)) | ((((i // step) & 3) ^ mask) * step))
                        for i in range(count)
                    ]
                    parts.append(lax.ppermute(x, axis, pairs))
                x = (parts[0] + parts[1]) + (parts[2] + parts[3])
                step *= 4
            else:
                x = x + lax.ppermute(x, axis, [(i, i ^ step) for i in range(count)])
                step *= 2
    return x


def subspace_kernel(g_ref, v_ref, out_ref):
    batch = g_ref.shape[0]
    rank = v_ref.shape[1]
    nt = (((1,), (1,)), ((), ()))
    sub = lax.broadcasted_iota(jnp.int32, (rank, rank), 0)
    lane = lax.broadcasted_iota(jnp.int32, (rank, rank), 1)
    sub_wide = lax.broadcasted_iota(jnp.int32, v_ref.shape[1:], 0)
    grams = [g_ref[b] for b in range(batch)]
    currents = [v_ref[b] for b in range(batch)]
    for repeat in range(POWER):
        carry = []
        for b in range(batch):
            product = lax.dot_general(
                currents[b], grams[b], nt, precision=HIGHEST, preferred_element_type=jnp.float32
            )
            inner = lax.dot_general(product, product, nt, precision=HIGHEST, preferred_element_type=jnp.float32)
            carry.append((inner, product, jnp.zeros_like(product)))

        def one_column(j, carry):
            out = []
            for inner, rest, solved in carry:
                row = jnp.sum(jnp.where(sub == j, inner, 0.0), axis=0, keepdims=True)
                col = jnp.sum(jnp.where(lane == j, inner, 0.0), axis=1, keepdims=True)
                pivot = jnp.sum(jnp.where(lane[:1] == j, row, 0.0), axis=1, keepdims=True)
                scale = lax.rsqrt(pivot)
                factor_row = jnp.where(lane[:1] >= j, row * scale, 0.0)
                factor_col = jnp.where(sub[:, :1] >= j, col * scale, 0.0)
                inner = inner - factor_col * factor_row
                answer = jnp.sum(jnp.where(sub_wide == j, rest, 0.0), axis=0, keepdims=True) * scale
                rest = rest - factor_col * answer
                solved = jnp.where(sub_wide == j, answer, solved)
                out.append((inner, rest, solved))
            return tuple(out)

        carry = lax.fori_loop(0, rank, one_column, tuple(carry), unroll=True)
        currents = [solved for _, _, solved in carry]
    for b in range(batch):
        out_ref[b] = currents[b]


def subspace_batch(grams, starts_t):
    batch, size, _ = grams.shape
    rank = starts_t.shape[1]
    return pl.pallas_call(
        subspace_kernel,
        out_shape=jax.ShapeDtypeStruct((batch, rank, size), jnp.float32),
    )(grams, starts_t)


def fast_subspace(gram_matrix, start_block):
    return subspace_batch(gram_matrix[None], start_block.T[None])[0].T


def orthonormal(columns_block):
    inner_gram = jnp.dot(columns_block.T, columns_block, precision=HIGHEST)
    lower_factor = jnp.linalg.cholesky(inner_gram)
    return lax.linalg.triangular_solve(
        lower_factor, columns_block, left_side=False, lower=True, transpose_a=True
    )


def subspace(gram_matrix, start_block):
    current = start_block
    for repeat in range(POWER):
        current = orthonormal(jnp.dot(gram_matrix, current, precision=HIGHEST))
    return current


def coefficient_tree(full_gram, start_merge, rank_size, freq_count):
    pairs = freq_count // 2
    width = 2 * rank_size
    blocks = jnp.stack(
        [full_gram[p * width : (p + 1) * width, p * width : (p + 1) * width] for p in range(pairs)]
    )
    starts_t = jnp.broadcast_to(start_merge.T[None], (pairs,) + start_merge.T.shape)
    pair_weights = jnp.swapaxes(subspace_batch(blocks, starts_t), 1, 2)
    zero = jnp.zeros((width, rank_size), jnp.float32)
    coefficients = []
    for p in range(pairs):
        parts = [zero] * pairs
        parts[p] = pair_weights[p]
        coefficients.append(jnp.concatenate(parts, axis=0))
    while len(coefficients) > 1:
        merged = []
        for position in range(0, len(coefficients), 2):
            joined = jnp.concatenate([coefficients[position], coefficients[position + 1]], axis=1)
            pair_gram = jnp.dot(
                joined.T, jnp.dot(full_gram, joined, precision=HIGHEST), precision=HIGHEST
            )
            merged.append(jnp.dot(joined, fast_subspace(pair_gram, start_merge), precision=HIGHEST))
        coefficients = merged
    return coefficients[0]


def shards(snapshots, block_cols, mass_blocks, start_group, start_merge):
    block_size = mass_blocks.shape[2]
    local_blocks = block_cols.shape[0]
    local_cols = snapshots.shape[1]
    total_rows = lax.axis_size("rows") * snapshots.shape[0]
    width = HB * block_size
    count = lax.axis_size("rows")
    forward = [(i, i + 1) for i in range(count - 1)]
    backward = [(target, source) for source, target in forward]
    low = lax.ppermute(snapshots[snapshots.shape[0] - width :], "rows", forward)
    high = lax.ppermute(snapshots[:width], "rows", backward)
    local_index = block_cols - lax.axis_index("rows") * local_blocks + HB
    weighted, local_gram = apply_mass(low, snapshots, high, mass_blocks, local_index)
    group_gram = butterfly_sum(local_gram, ("rows",)) / total_rows
    weights = fast_subspace(group_gram, start_group)
    rank_size = weights.shape[1]
    freq_count = lax.axis_size("freq")
    group = lax.axis_index("freq")
    share = weighted.shape[0] // freq_count

    def modes_of(part):
        rows_part = lax.dynamic_slice_in_dim(weighted, part * share, share, 0)
        return lax.dot_general(weights, rows_part, (((0,), (1,)), ((), ())), precision=HIGH)

    received = [None] * freq_count
    back = [(i, (i - 1) % freq_count) for i in range(freq_count)]
    for shift in range(1, freq_count):
        piece = modes_of((group + shift) % freq_count)
        pairs = [(i, (i + shift) % freq_count) for i in range(freq_count)]
        if freq_count == 4 and shift == 2:
            half = piece.shape[1] // 2
            direct = lax.ppermute(piece[:, :half], "freq", pairs)
            relayed = lax.ppermute(lax.ppermute(piece[:, half:], "freq", back), "freq", back)
            received[shift] = jnp.concatenate([direct, relayed], axis=1)
        else:
            received[shift] = lax.ppermute(piece, "freq", pairs)
    received[0] = modes_of(group)
    stacked = jnp.concatenate(received, axis=0)
    source = (group - jnp.arange(freq_count)) % freq_count
    local_full = jnp.dot(stacked, stacked.T, precision=HIGH)
    blocked = local_full.reshape(freq_count, rank_size, freq_count, rank_size)
    blocked = jnp.take(jnp.take(blocked, source, axis=0), source, axis=2)
    full_gram = butterfly_sum(
        blocked.reshape(freq_count * rank_size, freq_count * rank_size), ("rows", "freq")
    ) / total_rows
    combined = coefficient_tree(full_gram, start_merge, rank_size, freq_count)
    shifted = jnp.take(combined.reshape(freq_count, rank_size, rank_size), source, axis=0)
    result = jnp.dot(shifted.reshape(freq_count * rank_size, rank_size).T, stacked, precision=HIGH)
    return result


def solution(mesh):
    in_specs = (
        P("rows", "freq"),
        P("rows", None),
        P("rows", None, None, None),
        P("freq", None),
        P(),
    )
    out_specs = P(None, ("rows", "freq"))
    return jax.shard_map(shards, mesh=mesh, in_specs=in_specs, out_specs=out_specs, check_vma=False)
```

```python
import jax
import jax.numpy as jnp
from jax import lax
from jax.sharding import PartitionSpec as P
from jax.experimental import pallas as pl
from jax.experimental.pallas import tpu as pltpu

HB = 2
POWER = 2


HIGHEST = lax.Precision.HIGHEST
HIGH = lax.Precision.HIGH


def extended_2(block, sides, width):
    for axis, dim in sides:
        count = lax.axis_size(axis)
        forward = [(i, i + 1) for i in range(count - 1)]
        backward = [(target, source) for source, target in forward]
        low = lax.ppermute(
            lax.slice_in_dim(block, block.shape[dim] - width, None, axis=dim), axis, forward
        )
        high = lax.ppermute(lax.slice_in_dim(block, 0, width, axis=dim), axis, backward)
        block = jnp.concatenate([low, block, high], axis=dim)
    return block


ROWS_PER_STEP = 16


def mass_kernel(index_ref, low_ref, own_ref, high_ref, mass_ref, out_ref, gram_ref):
    step = pl.program_id(0)
    size = mass_ref.shape[2]
    halo = low_ref.shape[0] // size
    own_tiles = own_ref.shape[0] // size
    rows_here = mass_ref.shape[0]
    kb = mass_ref.shape[1]

    @pl.when(step == 0)
    def _():
        gram_ref[...] = jnp.zeros(gram_ref.shape, gram_ref.dtype)

    for row in range(rows_here):
        block = step * rows_here + row
        tiles = []
        for k in range(kb):
            tile_id = index_ref[block * kb + k]
            own_at = jnp.clip(tile_id - halo, 0, own_tiles - 1)
            low_at = jnp.clip(tile_id, 0, halo - 1)
            high_at = jnp.clip(tile_id - halo - own_tiles, 0, halo - 1)
            own_tile = own_ref[pl.ds(pl.multiple_of(own_at * size, size), size), :]
            low_tile = low_ref[pl.ds(pl.multiple_of(low_at * size, size), size), :]
            high_tile = high_ref[pl.ds(pl.multiple_of(high_at * size, size), size), :]
            tile = jnp.where(
                tile_id < halo, low_tile, jnp.where(tile_id >= halo + own_tiles, high_tile, own_tile)
            )
            tiles.append(tile)
        joined_mass = jnp.concatenate([mass_ref[row, k] for k in range(kb)], axis=1)
        joined_tiles = jnp.concatenate(tiles, axis=0)
        out_ref[row * size : (row + 1) * size, :] = jnp.dot(
            joined_mass, joined_tiles, preferred_element_type=jnp.float32
        )

    chunk = out_ref[...]
    high_part = chunk.astype(jnp.bfloat16)
    low_part = (chunk - high_part.astype(jnp.float32)).astype(jnp.bfloat16)
    dims = (((0,), (0,)), ((), ()))
    main = lax.dot_general(high_part, high_part, dims, preferred_element_type=jnp.float32)
    cross = lax.dot_general(high_part, low_part, dims, preferred_element_type=jnp.float32)
    gram_ref[...] += main + (cross + cross.T)


def apply_mass(low, own, high, mass_blocks, tile_index):
    blocks, kb, size, _ = mass_blocks.shape
    cols = own.shape[1]
    per = ROWS_PER_STEP
    grid_spec = pltpu.PrefetchScalarGridSpec(
        num_scalar_prefetch=1,
        grid=(blocks // per,),
        in_specs=[
            pl.BlockSpec(low.shape, lambda i, idx: (0, 0)),
            pl.BlockSpec(own.shape, lambda i, idx: (0, 0)),
            pl.BlockSpec(high.shape, lambda i, idx: (0, 0)),
            pl.BlockSpec((per, kb, size, size), lambda i, idx: (i, 0, 0, 0)),
        ],
        out_specs=[
            pl.BlockSpec((per * size, cols), lambda i, idx: (i, 0)),
            pl.BlockSpec((cols, cols), lambda i, idx: (0, 0)),
        ],
    )
    return pl.pallas_call(
        mass_kernel,
        grid_spec=grid_spec,
        out_shape=[
            jax.ShapeDtypeStruct((blocks * size, cols), jnp.float32),
            jax.ShapeDtypeStruct((cols, cols), jnp.float32),
        ],
        compiler_params=pltpu.CompilerParams(dimension_semantics=("arbitrary",)),
    )(tile_index.reshape(-1), low, own, high, mass_blocks)


def butterfly_sum(x, axes):
    for axis in axes:
        count = lax.axis_size(axis)
        step = 1
        while step < count:
            if step * 4 <= count:
                parts = [x]
                for mask in (1, 2, 3):
                    pairs = [
                        (i, (i & ~(3 * step)) | ((((i // step) & 3) ^ mask) * step))
                        for i in range(count)
                    ]
                    parts.append(lax.ppermute(x, axis, pairs))
                x = (parts[0] + parts[1]) + (parts[2] + parts[3])
                step *= 4
            else:
                x = x + lax.ppermute(x, axis, [(i, i ^ step) for i in range(count)])
                step *= 2
    return x


def subspace_kernel(g_ref, v_ref, out_ref):
    batch = g_ref.shape[0]
    rank = v_ref.shape[1]
    nt = (((1,), (1,)), ((), ()))
    sub = lax.broadcasted_iota(jnp.int32, (rank, rank), 0)
    lane = lax.broadcasted_iota(jnp.int32, (rank, rank), 1)
    sub_wide = lax.broadcasted_iota(jnp.int32, v_ref.shape[1:], 0)
    grams = [g_ref[b] for b in range(batch)]
    currents = [v_ref[b] for b in range(batch)]
    for repeat in range(POWER):
        carry = []
        for b in range(batch):
            product = lax.dot_general(
                currents[b], grams[b], nt, precision=HIGHEST, preferred_element_type=jnp.float32
            )
            inner = lax.dot_general(product, product, nt, precision=HIGHEST, preferred_element_type=jnp.float32)
            carry.append((inner, product, jnp.zeros_like(product)))

        def one_column(j, carry):
            out = []
            for inner, rest, solved in carry:
                row = jnp.sum(jnp.where(sub == j, inner, 0.0), axis=0, keepdims=True)
                col = jnp.sum(jnp.where(lane == j, inner, 0.0), axis=1, keepdims=True)
                pivot = jnp.sum(jnp.where(lane[:1] == j, row, 0.0), axis=1, keepdims=True)
                scale = lax.rsqrt(pivot)
                factor_row = jnp.where(lane[:1] >= j, row * scale, 0.0)
                factor_col = jnp.where(sub[:, :1] >= j, col * scale, 0.0)
                inner = inner - factor_col * factor_row
                answer = jnp.sum(jnp.where(sub_wide == j, rest, 0.0), axis=0, keepdims=True) * scale
                rest = rest - factor_col * answer
                solved = jnp.where(sub_wide == j, answer, solved)
                out.append((inner, rest, solved))
            return tuple(out)

        carry = lax.fori_loop(0, rank, one_column, tuple(carry), unroll=True)
        currents = [solved for _, _, solved in carry]
    for b in range(batch):
        out_ref[b] = currents[b]


def subspace_batch(grams, starts_t):
    batch, size, _ = grams.shape
    rank = starts_t.shape[1]
    return pl.pallas_call(
        subspace_kernel,
        out_shape=jax.ShapeDtypeStruct((batch, rank, size), jnp.float32),
    )(grams, starts_t)


def fast_subspace(gram_matrix, start_block):
    return subspace_batch(gram_matrix[None], start_block.T[None])[0].T


def orthonormal(columns_block):
    inner_gram = jnp.dot(columns_block.T, columns_block, precision=HIGHEST)
    lower_factor = jnp.linalg.cholesky(inner_gram)
    return lax.linalg.triangular_solve(
        lower_factor, columns_block, left_side=False, lower=True, transpose_a=True
    )


def subspace(gram_matrix, start_block):
    current = start_block
    for repeat in range(POWER):
        current = orthonormal(jnp.dot(gram_matrix, current, precision=HIGHEST))
    return current


def coefficient_tree(full_gram, start_merge, rank_size, freq_count):
    pairs = freq_count // 2
    width = 2 * rank_size
    blocks = jnp.stack(
        [full_gram[p * width : (p + 1) * width, p * width : (p + 1) * width] for p in range(pairs)]
    )
    starts_t = jnp.broadcast_to(start_merge.T[None], (pairs,) + start_merge.T.shape)
    pair_weights = jnp.swapaxes(subspace_batch(blocks, starts_t), 1, 2)
    zero = jnp.zeros((width, rank_size), jnp.float32)
    coefficients = []
    for p in range(pairs):
        parts = [zero] * pairs
        parts[p] = pair_weights[p]
        coefficients.append(jnp.concatenate(parts, axis=0))
    while len(coefficients) > 1:
        merged = []
        for position in range(0, len(coefficients), 2):
            joined = jnp.concatenate([coefficients[position], coefficients[position + 1]], axis=1)
            pair_gram = jnp.dot(
                joined.T, jnp.dot(full_gram, joined, precision=HIGHEST), precision=HIGHEST
            )
            merged.append(jnp.dot(joined, fast_subspace(pair_gram, start_merge), precision=HIGHEST))
        coefficients = merged
    return coefficients[0]


def shards(snapshots, block_cols, mass_blocks, start_group, start_merge):
    block_size = mass_blocks.shape[2]
    local_blocks = block_cols.shape[0]
    local_cols = snapshots.shape[1]
    total_rows = lax.axis_size("rows") * snapshots.shape[0]
    width = HB * block_size
    count = lax.axis_size("rows")
    forward = [(i, i + 1) for i in range(count - 1)]
    backward = [(target, source) for source, target in forward]
    low = lax.ppermute(snapshots[snapshots.shape[0] - width :], "rows", forward)
    high = lax.ppermute(snapshots[:width], "rows", backward)
    local_index = block_cols - lax.axis_index("rows") * local_blocks + HB
    weighted, local_gram = apply_mass(low, snapshots, high, mass_blocks, local_index)
    group_gram = butterfly_sum(local_gram, ("rows",)) / total_rows
    weights = fast_subspace(group_gram, start_group)
    rank_size = weights.shape[1]
    freq_count = lax.axis_size("freq")
    group = lax.axis_index("freq")
    share = weighted.shape[0] // freq_count

    def modes_of(part):
        rows_part = lax.dynamic_slice_in_dim(weighted, part * share, share, 0)
        return lax.dot_general(weights, rows_part, (((0,), (1,)), ((), ())), precision=HIGH)

    received = [None] * freq_count
    for shift in range(1, freq_count):
        piece = modes_of((group + shift) % freq_count)
        pairs = [(i, (i + shift) % freq_count) for i in range(freq_count)]
        received[shift] = lax.ppermute(piece, "freq", pairs)
    received[0] = modes_of(group)
    stacked = jnp.concatenate(received, axis=0)
    source = (group - jnp.arange(freq_count)) % freq_count
    local_full = jnp.dot(stacked, stacked.T, precision=HIGH)
    blocked = local_full.reshape(freq_count, rank_size, freq_count, rank_size)
    blocked = jnp.take(jnp.take(blocked, source, axis=0), source, axis=2)
    full_gram = butterfly_sum(
        blocked.reshape(freq_count * rank_size, freq_count * rank_size), ("rows", "freq")
    ) / total_rows
    combined = coefficient_tree(full_gram, start_merge, rank_size, freq_count)
    shifted = jnp.take(combined.reshape(freq_count, rank_size, rank_size), source, axis=0)
    result = jnp.dot(shifted.reshape(freq_count * rank_size, rank_size).T, stacked, precision=HIGH)
    return result


def solution(mesh):
    in_specs = (
        P("rows", "freq"),
        P("rows", None),
        P("rows", None, None, None),
        P("freq", None),
        P(),
    )
    out_specs = P(None, ("rows", "freq"))
    return jax.shard_map(shards, mesh=mesh, in_specs=in_specs, out_specs=out_specs, check_vma=False)
```

```python
import jax
import jax.numpy as jnp
from jax import lax
from jax.sharding import PartitionSpec as P
from jax.experimental import pallas as pl
from jax.experimental.pallas import tpu as pltpu

HB = 2
POWER = 2


HIGHEST = lax.Precision.HIGHEST
HIGH = lax.Precision.HIGH


def extended_2(block, sides, width):
    for axis, dim in sides:
        count = lax.axis_size(axis)
        forward = [(i, i + 1) for i in range(count - 1)]
        backward = [(target, source) for source, target in forward]
        low = lax.ppermute(
            lax.slice_in_dim(block, block.shape[dim] - width, None, axis=dim), axis, forward
        )
        high = lax.ppermute(lax.slice_in_dim(block, 0, width, axis=dim), axis, backward)
        block = jnp.concatenate([low, block, high], axis=dim)
    return block


ROWS_PER_STEP = 16


def mass_kernel(index_ref, low_ref, own_ref, high_ref, mass_ref, out_ref, gram_ref):
    step = pl.program_id(0)
    size = mass_ref.shape[2]
    halo = low_ref.shape[0] // size
    own_tiles = own_ref.shape[0] // size
    rows_here = mass_ref.shape[0]
    kb = mass_ref.shape[1]

    @pl.when(step == 0)
    def _():
        gram_ref[...] = jnp.zeros(gram_ref.shape, gram_ref.dtype)

    for row in range(rows_here):
        block = step * rows_here + row
        tiles = []
        for k in range(kb):
            tile_id = index_ref[block * kb + k]
            own_at = jnp.clip(tile_id - halo, 0, own_tiles - 1)
            low_at = jnp.clip(tile_id, 0, halo - 1)
            high_at = jnp.clip(tile_id - halo - own_tiles, 0, halo - 1)
            own_tile = own_ref[pl.ds(pl.multiple_of(own_at * size, size), size), :]
            low_tile = low_ref[pl.ds(pl.multiple_of(low_at * size, size), size), :]
            high_tile = high_ref[pl.ds(pl.multiple_of(high_at * size, size), size), :]
            tile = jnp.where(
                tile_id < halo, low_tile, jnp.where(tile_id >= halo + own_tiles, high_tile, own_tile)
            )
            tiles.append(tile)
        joined_mass = jnp.concatenate([mass_ref[row, k] for k in range(kb)], axis=1)
        joined_tiles = jnp.concatenate(tiles, axis=0)
        out_ref[row * size : (row + 1) * size, :] = jnp.dot(
            joined_mass, joined_tiles, preferred_element_type=jnp.float32
        )

    chunk = out_ref[...]
    high_part = chunk.astype(jnp.bfloat16)
    low_part = (chunk - high_part.astype(jnp.float32)).astype(jnp.bfloat16)
    high_t = high_part.T
    main = jnp.dot(high_t, high_part, preferred_element_type=jnp.float32)
    cross = jnp.dot(high_t, low_part, preferred_element_type=jnp.float32)
    gram_ref[...] += main + (cross + cross.T)


def apply_mass(low, own, high, mass_blocks, tile_index):
    blocks, kb, size, _ = mass_blocks.shape
    cols = own.shape[1]
    per = ROWS_PER_STEP
    grid_spec = pltpu.PrefetchScalarGridSpec(
        num_scalar_prefetch=1,
        grid=(blocks // per,),
        in_specs=[
            pl.BlockSpec(low.shape, lambda i, idx: (0, 0)),
            pl.BlockSpec(own.shape, lambda i, idx: (0, 0)),
            pl.BlockSpec(high.shape, lambda i, idx: (0, 0)),
            pl.BlockSpec((per, kb, size, size), lambda i, idx: (i, 0, 0, 0)),
        ],
        out_specs=[
            pl.BlockSpec((per * size, cols), lambda i, idx: (i, 0)),
            pl.BlockSpec((cols, cols), lambda i, idx: (0, 0)),
        ],
    )
    return pl.pallas_call(
        mass_kernel,
        grid_spec=grid_spec,
        out_shape=[
            jax.ShapeDtypeStruct((blocks * size, cols), jnp.float32),
            jax.ShapeDtypeStruct((cols, cols), jnp.float32),
        ],
        compiler_params=pltpu.CompilerParams(dimension_semantics=("arbitrary",)),
    )(tile_index.reshape(-1), low, own, high, mass_blocks)


def butterfly_sum(x, axes):
    for axis in axes:
        count = lax.axis_size(axis)
        step = 1
        while step < count:
            if step * 4 <= count:
                parts = [x]
                for mask in (1, 2, 3):
                    pairs = [
                        (i, (i & ~(3 * step)) | ((((i // step) & 3) ^ mask) * step))
                        for i in range(count)
                    ]
                    parts.append(lax.ppermute(x, axis, pairs))
                x = (parts[0] + parts[1]) + (parts[2] + parts[3])
                step *= 4
            else:
                x = x + lax.ppermute(x, axis, [(i, i ^ step) for i in range(count)])
                step *= 2
    return x


def subspace_kernel(g_ref, v_ref, out_ref):
    batch = g_ref.shape[0]
    rank = v_ref.shape[1]
    nt = (((1,), (1,)), ((), ()))
    sub = lax.broadcasted_iota(jnp.int32, (rank, rank), 0)
    lane = lax.broadcasted_iota(jnp.int32, (rank, rank), 1)
    sub_wide = lax.broadcasted_iota(jnp.int32, v_ref.shape[1:], 0)
    grams = [g_ref[b] for b in range(batch)]
    currents = [v_ref[b] for b in range(batch)]
    for repeat in range(POWER):
        carry = []
        for b in range(batch):
            product = lax.dot_general(
                currents[b], grams[b], nt, precision=HIGHEST, preferred_element_type=jnp.float32
            )
            inner = lax.dot_general(product, product, nt, precision=HIGHEST, preferred_element_type=jnp.float32)
            carry.append((inner, product, jnp.zeros_like(product)))

        def one_column(j, carry):
            out = []
            for inner, rest, solved in carry:
                row = jnp.sum(jnp.where(sub == j, inner, 0.0), axis=0, keepdims=True)
                col = jnp.sum(jnp.where(lane == j, inner, 0.0), axis=1, keepdims=True)
                pivot = jnp.sum(jnp.where(lane[:1] == j, row, 0.0), axis=1, keepdims=True)
                scale = lax.rsqrt(pivot)
                factor_row = jnp.where(lane[:1] >= j, row * scale, 0.0)
                factor_col = jnp.where(sub[:, :1] >= j, col * scale, 0.0)
                inner = inner - factor_col * factor_row
                answer = jnp.sum(jnp.where(sub_wide == j, rest, 0.0), axis=0, keepdims=True) * scale
                rest = rest - factor_col * answer
                solved = jnp.where(sub_wide == j, answer, solved)
                out.append((inner, rest, solved))
            return tuple(out)

        carry = lax.fori_loop(0, rank, one_column, tuple(carry), unroll=True)
        currents = [solved for _, _, solved in carry]
    for b in range(batch):
        out_ref[b] = currents[b]


def subspace_batch(grams, starts_t):
    batch, size, _ = grams.shape
    rank = starts_t.shape[1]
    return pl.pallas_call(
        subspace_kernel,
        out_shape=jax.ShapeDtypeStruct((batch, rank, size), jnp.float32),
    )(grams, starts_t)


def fast_subspace(gram_matrix, start_block):
    return subspace_batch(gram_matrix[None], start_block.T[None])[0].T


def orthonormal(columns_block):
    inner_gram = jnp.dot(columns_block.T, columns_block, precision=HIGHEST)
    lower_factor = jnp.linalg.cholesky(inner_gram)
    return lax.linalg.triangular_solve(
        lower_factor, columns_block, left_side=False, lower=True, transpose_a=True
    )


def subspace(gram_matrix, start_block):
    current = start_block
    for repeat in range(POWER):
        current = orthonormal(jnp.dot(gram_matrix, current, precision=HIGHEST))
    return current


def coefficient_tree(full_gram, start_merge, rank_size, freq_count):
    pairs = freq_count // 2
    width = 2 * rank_size
    blocks = jnp.stack(
        [full_gram[p * width : (p + 1) * width, p * width : (p + 1) * width] for p in range(pairs)]
    )
    starts_t = jnp.broadcast_to(start_merge.T[None], (pairs,) + start_merge.T.shape)
    pair_weights = jnp.swapaxes(subspace_batch(blocks, starts_t), 1, 2)
    zero = jnp.zeros((width, rank_size), jnp.float32)
    coefficients = []
    for p in range(pairs):
        parts = [zero] * pairs
        parts[p] = pair_weights[p]
        coefficients.append(jnp.concatenate(parts, axis=0))
    while len(coefficients) > 1:
        merged = []
        for position in range(0, len(coefficients), 2):
            joined = jnp.concatenate([coefficients[position], coefficients[position + 1]], axis=1)
            pair_gram = jnp.dot(
                joined.T, jnp.dot(full_gram, joined, precision=HIGHEST), precision=HIGHEST
            )
            merged.append(jnp.dot(joined, fast_subspace(pair_gram, start_merge), precision=HIGHEST))
        coefficients = merged
    return coefficients[0]


def shards(snapshots, block_cols, mass_blocks, start_group, start_merge):
    block_size = mass_blocks.shape[2]
    local_blocks = block_cols.shape[0]
    local_cols = snapshots.shape[1]
    total_rows = lax.axis_size("rows") * snapshots.shape[0]
    width = HB * block_size
    count = lax.axis_size("rows")
    forward = [(i, i + 1) for i in range(count - 1)]
    backward = [(target, source) for source, target in forward]
    low = lax.ppermute(snapshots[snapshots.shape[0] - width :], "rows", forward)
    high = lax.ppermute(snapshots[:width], "rows", backward)
    local_index = block_cols - lax.axis_index("rows") * local_blocks + HB
    weighted, local_gram = apply_mass(low, snapshots, high, mass_blocks, local_index)
    group_gram = butterfly_sum(local_gram, ("rows",)) / total_rows
    weights = fast_subspace(group_gram, start_group)
    rank_size = weights.shape[1]
    freq_count = lax.axis_size("freq")
    group = lax.axis_index("freq")
    share = weighted.shape[0] // freq_count

    def modes_of(part):
        rows_part = lax.dynamic_slice_in_dim(weighted, part * share, share, 0)
        return lax.dot_general(weights, rows_part, (((0,), (1,)), ((), ())), precision=HIGH)

    received = [None] * freq_count
    for shift in range(1, freq_count):
        piece = modes_of((group + shift) % freq_count)
        pairs = [(i, (i + shift) % freq_count) for i in range(freq_count)]
        received[shift] = lax.ppermute(piece, "freq", pairs)
    received[0] = modes_of(group)
    stacked = jnp.concatenate(received, axis=0)
    source = (group - jnp.arange(freq_count)) % freq_count
    local_full = jnp.dot(stacked, stacked.T, precision=HIGH)
    blocked = local_full.reshape(freq_count, rank_size, freq_count, rank_size)
    blocked = jnp.take(jnp.take(blocked, source, axis=0), source, axis=2)
    full_gram = butterfly_sum(
        blocked.reshape(freq_count * rank_size, freq_count * rank_size), ("rows", "freq")
    ) / total_rows
    combined = coefficient_tree(full_gram, start_merge, rank_size, freq_count)
    shifted = jnp.take(combined.reshape(freq_count, rank_size, rank_size), source, axis=0)
    result = jnp.dot(shifted.reshape(freq_count * rank_size, rank_size).T, stacked, precision=HIGH)
    return result


def solution(mesh):
    in_specs = (
        P("rows", "freq"),
        P("rows", None),
        P("rows", None, None, None),
        P("freq", None),
        P(),
    )
    out_specs = P(None, ("rows", "freq"))
    return jax.shard_map(shards, mesh=mesh, in_specs=in_specs, out_specs=out_specs, check_vma=False)
```

```python
import jax
import jax.numpy as jnp
from jax import lax
from jax.sharding import PartitionSpec as P
from jax.experimental import pallas as pl
from jax.experimental.pallas import tpu as pltpu

HB = 2
POWER = 2


HIGHEST = lax.Precision.HIGHEST
HIGH = lax.Precision.HIGH


def extended_2(block, sides, width):
    for axis, dim in sides:
        count = lax.axis_size(axis)
        forward = [(i, i + 1) for i in range(count - 1)]
        backward = [(target, source) for source, target in forward]
        low = lax.ppermute(
            lax.slice_in_dim(block, block.shape[dim] - width, None, axis=dim), axis, forward
        )
        high = lax.ppermute(lax.slice_in_dim(block, 0, width, axis=dim), axis, backward)
        block = jnp.concatenate([low, block, high], axis=dim)
    return block


ROWS_PER_STEP = 16


def mass_kernel(index_ref, low_ref, own_ref, high_ref, mass_ref, out_ref, gram_ref):
    step = pl.program_id(0)
    size = mass_ref.shape[2]
    halo = low_ref.shape[0] // size
    own_tiles = own_ref.shape[0] // size
    rows_here = mass_ref.shape[0]
    kb = mass_ref.shape[1]

    @pl.when(step == 0)
    def _():
        gram_ref[...] = jnp.zeros(gram_ref.shape, gram_ref.dtype)

    for row in range(rows_here):
        block = step * rows_here + row
        total = jnp.zeros((size, out_ref.shape[1]), jnp.float32)
        for k in range(kb):
            tile_id = index_ref[block * kb + k]
            own_at = jnp.clip(tile_id - halo, 0, own_tiles - 1)
            low_at = jnp.clip(tile_id, 0, halo - 1)
            high_at = jnp.clip(tile_id - halo - own_tiles, 0, halo - 1)
            own_tile = own_ref[pl.ds(pl.multiple_of(own_at * size, size), size), :]
            low_tile = low_ref[pl.ds(pl.multiple_of(low_at * size, size), size), :]
            high_tile = high_ref[pl.ds(pl.multiple_of(high_at * size, size), size), :]
            tile = jnp.where(
                tile_id < halo, low_tile, jnp.where(tile_id >= halo + own_tiles, high_tile, own_tile)
            )
            total = total + jnp.dot(mass_ref[row, k], tile, preferred_element_type=jnp.float32)
        out_ref[row * size : (row + 1) * size, :] = total

    chunk = out_ref[...]
    high_part = chunk.astype(jnp.bfloat16)
    low_part = (chunk - high_part.astype(jnp.float32)).astype(jnp.bfloat16)
    dims = (((0,), (0,)), ((), ()))
    main = lax.dot_general(high_part, high_part, dims, preferred_element_type=jnp.float32)
    cross = lax.dot_general(high_part, low_part, dims, preferred_element_type=jnp.float32)
    gram_ref[...] += main + (cross + cross.T)


def apply_mass(low, own, high, mass_blocks, tile_index):
    blocks, kb, size, _ = mass_blocks.shape
    cols = own.shape[1]
    per = ROWS_PER_STEP
    grid_spec = pltpu.PrefetchScalarGridSpec(
        num_scalar_prefetch=1,
        grid=(blocks // per,),
        in_specs=[
            pl.BlockSpec(low.shape, lambda i, idx: (0, 0)),
            pl.BlockSpec(own.shape, lambda i, idx: (0, 0)),
            pl.BlockSpec(high.shape, lambda i, idx: (0, 0)),
            pl.BlockSpec((per, kb, size, size), lambda i, idx: (i, 0, 0, 0)),
        ],
        out_specs=[
            pl.BlockSpec((per * size, cols), lambda i, idx: (i, 0)),
            pl.BlockSpec((cols, cols), lambda i, idx: (0, 0)),
        ],
    )
    return pl.pallas_call(
        mass_kernel,
        grid_spec=grid_spec,
        out_shape=[
            jax.ShapeDtypeStruct((blocks * size, cols), jnp.float32),
            jax.ShapeDtypeStruct((cols, cols), jnp.float32),
        ],
        compiler_params=pltpu.CompilerParams(dimension_semantics=("arbitrary",)),
    )(tile_index.reshape(-1), low, own, high, mass_blocks)


def butterfly_sum(x, axes):
    for axis in axes:
        count = lax.axis_size(axis)
        step = 1
        while step < count:
            if step * 4 <= count:
                parts = [x]
                for mask in (1, 2, 3):
                    pairs = [
                        (i, (i & ~(3 * step)) | ((((i // step) & 3) ^ mask) * step))
                        for i in range(count)
                    ]
                    parts.append(lax.ppermute(x, axis, pairs))
                x = (parts[0] + parts[1]) + (parts[2] + parts[3])
                step *= 4
            else:
                x = x + lax.ppermute(x, axis, [(i, i ^ step) for i in range(count)])
                step *= 2
    return x


def subspace_kernel(g_ref, v_ref, out_ref):
    batch = g_ref.shape[0]
    rank = v_ref.shape[1]
    nt = (((1,), (1,)), ((), ()))
    sub = lax.broadcasted_iota(jnp.int32, (rank, rank), 0)
    lane = lax.broadcasted_iota(jnp.int32, (rank, rank), 1)
    sub_wide = lax.broadcasted_iota(jnp.int32, v_ref.shape[1:], 0)
    grams = [g_ref[b] for b in range(batch)]
    currents = [v_ref[b] for b in range(batch)]
    for repeat in range(POWER):
        carry = []
        for b in range(batch):
            product = lax.dot_general(
                currents[b], grams[b], nt, precision=HIGH, preferred_element_type=jnp.float32
            )
            inner = lax.dot_general(product, product, nt, precision=HIGH, preferred_element_type=jnp.float32)
            carry.append((inner, product, jnp.zeros_like(product)))

        def one_column(j, carry):
            out = []
            for inner, rest, solved in carry:
                row = jnp.sum(jnp.where(sub == j, inner, 0.0), axis=0, keepdims=True)
                col = jnp.sum(jnp.where(lane == j, inner, 0.0), axis=1, keepdims=True)
                pivot = jnp.sum(jnp.where(lane[:1] == j, row, 0.0), axis=1, keepdims=True)
                scale = lax.rsqrt(pivot)
                factor_row = jnp.where(lane[:1] >= j, row * scale, 0.0)
                factor_col = jnp.where(sub[:, :1] >= j, col * scale, 0.0)
                inner = inner - factor_col * factor_row
                answer = jnp.sum(jnp.where(sub_wide == j, rest, 0.0), axis=0, keepdims=True) * scale
                rest = rest - factor_col * answer
                solved = jnp.where(sub_wide == j, answer, solved)
                out.append((inner, rest, solved))
            return tuple(out)

        carry = lax.fori_loop(0, rank, one_column, tuple(carry), unroll=True)
        currents = [solved for _, _, solved in carry]
    for b in range(batch):
        out_ref[b] = currents[b]


def subspace_batch(grams, starts_t):
    batch, size, _ = grams.shape
    rank = starts_t.shape[1]
    return pl.pallas_call(
        subspace_kernel,
        out_shape=jax.ShapeDtypeStruct((batch, rank, size), jnp.float32),
    )(grams, starts_t)


def fast_subspace(gram_matrix, start_block):
    return subspace_batch(gram_matrix[None], start_block.T[None])[0].T


def orthonormal(columns_block):
    inner_gram = jnp.dot(columns_block.T, columns_block, precision=HIGHEST)
    lower_factor = jnp.linalg.cholesky(inner_gram)
    return lax.linalg.triangular_solve(
        lower_factor, columns_block, left_side=False, lower=True, transpose_a=True
    )


def subspace(gram_matrix, start_block):
    current = start_block
    for repeat in range(POWER):
        current = orthonormal(jnp.dot(gram_matrix, current, precision=HIGHEST))
    return current


def coefficient_tree(full_gram, start_merge, rank_size, freq_count):
    pairs = freq_count // 2
    width = 2 * rank_size
    blocks = jnp.stack(
        [full_gram[p * width : (p + 1) * width, p * width : (p + 1) * width] for p in range(pairs)]
    )
    starts_t = jnp.broadcast_to(start_merge.T[None], (pairs,) + start_merge.T.shape)
    pair_weights = jnp.swapaxes(subspace_batch(blocks, starts_t), 1, 2)
    zero = jnp.zeros((width, rank_size), jnp.float32)
    coefficients = []
    for p in range(pairs):
        parts = [zero] * pairs
        parts[p] = pair_weights[p]
        coefficients.append(jnp.concatenate(parts, axis=0))
    while len(coefficients) > 1:
        merged = []
        for position in range(0, len(coefficients), 2):
            joined = jnp.concatenate([coefficients[position], coefficients[position + 1]], axis=1)
            pair_gram = jnp.dot(
                joined.T, jnp.dot(full_gram, joined, precision=HIGHEST), precision=HIGHEST
            )
            merged.append(jnp.dot(joined, fast_subspace(pair_gram, start_merge), precision=HIGHEST))
        coefficients = merged
    return coefficients[0]


def shards(snapshots, block_cols, mass_blocks, start_group, start_merge):
    block_size = mass_blocks.shape[2]
    local_blocks = block_cols.shape[0]
    local_cols = snapshots.shape[1]
    total_rows = lax.axis_size("rows") * snapshots.shape[0]
    width = HB * block_size
    count = lax.axis_size("rows")
    forward = [(i, i + 1) for i in range(count - 1)]
    backward = [(target, source) for source, target in forward]
    low = lax.ppermute(snapshots[snapshots.shape[0] - width :], "rows", forward)
    high = lax.ppermute(snapshots[:width], "rows", backward)
    local_index = block_cols - lax.axis_index("rows") * local_blocks + HB
    weighted, local_gram = apply_mass(low, snapshots, high, mass_blocks, local_index)
    group_gram = butterfly_sum(local_gram, ("rows",)) / total_rows
    weights = fast_subspace(group_gram, start_group)
    rank_size = weights.shape[1]
    freq_count = lax.axis_size("freq")
    group = lax.axis_index("freq")
    share = weighted.shape[0] // freq_count

    def modes_of(part):
        rows_part = lax.dynamic_slice_in_dim(weighted, part * share, share, 0)
        return lax.dot_general(weights, rows_part, (((0,), (1,)), ((), ())), precision=HIGH)

    received = [None] * freq_count
    for shift in range(1, freq_count):
        piece = modes_of((group + shift) % freq_count)
        pairs = [(i, (i + shift) % freq_count) for i in range(freq_count)]
        received[shift] = lax.ppermute(piece, "freq", pairs)
    received[0] = modes_of(group)
    stacked = jnp.concatenate(received, axis=0)
    source = (group - jnp.arange(freq_count)) % freq_count
    local_full = jnp.dot(stacked, stacked.T, precision=HIGH)
    blocked = local_full.reshape(freq_count, rank_size, freq_count, rank_size)
    blocked = jnp.take(jnp.take(blocked, source, axis=0), source, axis=2)
    full_gram = butterfly_sum(
        blocked.reshape(freq_count * rank_size, freq_count * rank_size), ("rows", "freq")
    ) / total_rows
    combined = coefficient_tree(full_gram, start_merge, rank_size, freq_count)
    shifted = jnp.take(combined.reshape(freq_count, rank_size, rank_size), source, axis=0)
    result = jnp.dot(shifted.reshape(freq_count * rank_size, rank_size).T, stacked, precision=HIGH)
    return result


def solution(mesh):
    in_specs = (
        P("rows", "freq"),
        P("rows", None),
        P("rows", None, None, None),
        P("freq", None),
        P(),
    )
    out_specs = P(None, ("rows", "freq"))
    return jax.shard_map(shards, mesh=mesh, in_specs=in_specs, out_specs=out_specs, check_vma=False)
```

```python
import jax
import jax.numpy as jnp
from jax import lax
from jax.sharding import PartitionSpec as P
from jax.experimental import pallas as pl
from jax.experimental.pallas import tpu as pltpu

HB = 2
POWER = 2


HIGHEST = lax.Precision.HIGHEST
HIGH = lax.Precision.HIGH


def extended_2(block, sides, width):
    for axis, dim in sides:
        count = lax.axis_size(axis)
        forward = [(i, i + 1) for i in range(count - 1)]
        backward = [(target, source) for source, target in forward]
        low = lax.ppermute(
            lax.slice_in_dim(block, block.shape[dim] - width, None, axis=dim), axis, forward
        )
        high = lax.ppermute(lax.slice_in_dim(block, 0, width, axis=dim), axis, backward)
        block = jnp.concatenate([low, block, high], axis=dim)
    return block


ROWS_PER_STEP = 32


def mass_kernel(index_ref, low_ref, own_ref, high_ref, mass_ref, out_ref, gram_ref):
    step = pl.program_id(0)
    size = mass_ref.shape[2]
    halo = low_ref.shape[0] // size
    own_tiles = own_ref.shape[0] // size
    rows_here = mass_ref.shape[0]
    kb = mass_ref.shape[1]

    @pl.when(step == 0)
    def _():
        gram_ref[...] = jnp.zeros(gram_ref.shape, gram_ref.dtype)

    for row in range(rows_here):
        block = step * rows_here + row
        total = jnp.zeros((size, out_ref.shape[1]), jnp.float32)
        for k in range(kb):
            tile_id = index_ref[block * kb + k]
            own_at = jnp.clip(tile_id - halo, 0, own_tiles - 1)
            low_at = jnp.clip(tile_id, 0, halo - 1)
            high_at = jnp.clip(tile_id - halo - own_tiles, 0, halo - 1)
            own_tile = own_ref[pl.ds(pl.multiple_of(own_at * size, size), size), :]
            low_tile = low_ref[pl.ds(pl.multiple_of(low_at * size, size), size), :]
            high_tile = high_ref[pl.ds(pl.multiple_of(high_at * size, size), size), :]
            tile = jnp.where(
                tile_id < halo, low_tile, jnp.where(tile_id >= halo + own_tiles, high_tile, own_tile)
            )
            total = total + jnp.dot(mass_ref[row, k], tile, preferred_element_type=jnp.float32)
        out_ref[row * size : (row + 1) * size, :] = total

    chunk = out_ref[...]
    high_part = chunk.astype(jnp.bfloat16)
    low_part = (chunk - high_part.astype(jnp.float32)).astype(jnp.bfloat16)
    dims = (((0,), (0,)), ((), ()))
    main = lax.dot_general(high_part, high_part, dims, preferred_element_type=jnp.float32)
    cross = lax.dot_general(high_part, low_part, dims, preferred_element_type=jnp.float32)
    gram_ref[...] += main + (cross + cross.T)


def apply_mass(low, own, high, mass_blocks, tile_index):
    blocks, kb, size, _ = mass_blocks.shape
    cols = own.shape[1]
    per = ROWS_PER_STEP
    grid_spec = pltpu.PrefetchScalarGridSpec(
        num_scalar_prefetch=1,
        grid=(blocks // per,),
        in_specs=[
            pl.BlockSpec(low.shape, lambda i, idx: (0, 0)),
            pl.BlockSpec(own.shape, lambda i, idx: (0, 0)),
            pl.BlockSpec(high.shape, lambda i, idx: (0, 0)),
            pl.BlockSpec((per, kb, size, size), lambda i, idx: (i, 0, 0, 0)),
        ],
        out_specs=[
            pl.BlockSpec((per * size, cols), lambda i, idx: (i, 0)),
            pl.BlockSpec((cols, cols), lambda i, idx: (0, 0)),
        ],
    )
    return pl.pallas_call(
        mass_kernel,
        grid_spec=grid_spec,
        out_shape=[
            jax.ShapeDtypeStruct((blocks * size, cols), jnp.float32),
            jax.ShapeDtypeStruct((cols, cols), jnp.float32),
        ],
        compiler_params=pltpu.CompilerParams(dimension_semantics=("arbitrary",)),
    )(tile_index.reshape(-1), low, own, high, mass_blocks)


def butterfly_sum(x, axes):
    for axis in axes:
        count = lax.axis_size(axis)
        step = 1
        while step < count:
            if step * 4 <= count:
                parts = [x]
                for mask in (1, 2, 3):
                    pairs = [
                        (i, (i & ~(3 * step)) | ((((i // step) & 3) ^ mask) * step))
                        for i in range(count)
                    ]
                    parts.append(lax.ppermute(x, axis, pairs))
                x = (parts[0] + parts[1]) + (parts[2] + parts[3])
                step *= 4
            else:
                x = x + lax.ppermute(x, axis, [(i, i ^ step) for i in range(count)])
                step *= 2
    return x


def subspace_kernel(g_ref, v_ref, out_ref):
    batch = g_ref.shape[0]
    rank = v_ref.shape[1]
    nt = (((1,), (1,)), ((), ()))
    sub = lax.broadcasted_iota(jnp.int32, (rank, rank), 0)
    lane = lax.broadcasted_iota(jnp.int32, (rank, rank), 1)
    sub_wide = lax.broadcasted_iota(jnp.int32, v_ref.shape[1:], 0)
    grams = [g_ref[b] for b in range(batch)]
    currents = [v_ref[b] for b in range(batch)]
    for repeat in range(POWER):
        carry = []
        for b in range(batch):
            product = lax.dot_general(
                currents[b], grams[b], nt, precision=HIGHEST, preferred_element_type=jnp.float32
            )
            inner = lax.dot_general(product, product, nt, precision=HIGHEST, preferred_element_type=jnp.float32)
            carry.append((inner, product, jnp.zeros_like(product)))

        def one_column(j, carry):
            out = []
            for inner, rest, solved in carry:
                row = jnp.sum(jnp.where(sub == j, inner, 0.0), axis=0, keepdims=True)
                col = jnp.sum(jnp.where(lane == j, inner, 0.0), axis=1, keepdims=True)
                pivot = jnp.sum(jnp.where(lane[:1] == j, row, 0.0), axis=1, keepdims=True)
                scale = lax.rsqrt(pivot)
                factor_row = jnp.where(lane[:1] >= j, row * scale, 0.0)
                factor_col = jnp.where(sub[:, :1] >= j, col * scale, 0.0)
                inner = inner - factor_col * factor_row
                answer = jnp.sum(jnp.where(sub_wide == j, rest, 0.0), axis=0, keepdims=True) * scale
                rest = rest - factor_col * answer
                solved = jnp.where(sub_wide == j, answer, solved)
                out.append((inner, rest, solved))
            return tuple(out)

        carry = lax.fori_loop(0, rank, one_column, tuple(carry), unroll=True)
        currents = [solved for _, _, solved in carry]
    for b in range(batch):
        out_ref[b] = currents[b]


def subspace_batch(grams, starts_t):
    batch, size, _ = grams.shape
    rank = starts_t.shape[1]
    return pl.pallas_call(
        subspace_kernel,
        out_shape=jax.ShapeDtypeStruct((batch, rank, size), jnp.float32),
    )(grams, starts_t)


def fast_subspace(gram_matrix, start_block):
    return subspace_batch(gram_matrix[None], start_block.T[None])[0].T


def orthonormal(columns_block):
    inner_gram = jnp.dot(columns_block.T, columns_block, precision=HIGHEST)
    lower_factor = jnp.linalg.cholesky(inner_gram)
    return lax.linalg.triangular_solve(
        lower_factor, columns_block, left_side=False, lower=True, transpose_a=True
    )


def subspace(gram_matrix, start_block):
    current = start_block
    for repeat in range(POWER):
        current = orthonormal(jnp.dot(gram_matrix, current, precision=HIGHEST))
    return current


def coefficient_tree(full_gram, start_merge, rank_size, freq_count):
    pairs = freq_count // 2
    width = 2 * rank_size
    blocks = jnp.stack(
        [full_gram[p * width : (p + 1) * width, p * width : (p + 1) * width] for p in range(pairs)]
    )
    starts_t = jnp.broadcast_to(start_merge.T[None], (pairs,) + start_merge.T.shape)
    pair_weights = jnp.swapaxes(subspace_batch(blocks, starts_t), 1, 2)
    zero = jnp.zeros((width, rank_size), jnp.float32)
    coefficients = []
    for p in range(pairs):
        parts = [zero] * pairs
        parts[p] = pair_weights[p]
        coefficients.append(jnp.concatenate(parts, axis=0))
    while len(coefficients) > 1:
        merged = []
        for position in range(0, len(coefficients), 2):
            joined = jnp.concatenate([coefficients[position], coefficients[position + 1]], axis=1)
            pair_gram = jnp.dot(
                joined.T, jnp.dot(full_gram, joined, precision=HIGHEST), precision=HIGHEST
            )
            merged.append(jnp.dot(joined, fast_subspace(pair_gram, start_merge), precision=HIGHEST))
        coefficients = merged
    return coefficients[0]


def shards(snapshots, block_cols, mass_blocks, start_group, start_merge):
    block_size = mass_blocks.shape[2]
    local_blocks = block_cols.shape[0]
    local_cols = snapshots.shape[1]
    total_rows = lax.axis_size("rows") * snapshots.shape[0]
    width = HB * block_size
    count = lax.axis_size("rows")
    forward = [(i, i + 1) for i in range(count - 1)]
    backward = [(target, source) for source, target in forward]
    low = lax.ppermute(snapshots[snapshots.shape[0] - width :], "rows", forward)
    high = lax.ppermute(snapshots[:width], "rows", backward)
    local_index = block_cols - lax.axis_index("rows") * local_blocks + HB
    weighted, local_gram = apply_mass(low, snapshots, high, mass_blocks, local_index)
    group_gram = butterfly_sum(local_gram, ("rows",)) / total_rows
    weights = fast_subspace(group_gram, start_group)
    rank_size = weights.shape[1]
    freq_count = lax.axis_size("freq")
    group = lax.axis_index("freq")
    share = weighted.shape[0] // freq_count

    def modes_of(part):
        rows_part = lax.dynamic_slice_in_dim(weighted, part * share, share, 0)
        return lax.dot_general(weights, rows_part, (((0,), (1,)), ((), ())), precision=HIGH)

    received = [None] * freq_count
    for shift in range(1, freq_count):
        piece = modes_of((group + shift) % freq_count)
        pairs = [(i, (i + shift) % freq_count) for i in range(freq_count)]
        received[shift] = lax.ppermute(piece, "freq", pairs)
    received[0] = modes_of(group)
    stacked = jnp.concatenate(received, axis=0)
    source = (group - jnp.arange(freq_count)) % freq_count
    local_full = jnp.dot(stacked, stacked.T, precision=HIGH)
    blocked = local_full.reshape(freq_count, rank_size, freq_count, rank_size)
    blocked = jnp.take(jnp.take(blocked, source, axis=0), source, axis=2)
    full_gram = butterfly_sum(
        blocked.reshape(freq_count * rank_size, freq_count * rank_size), ("rows", "freq")
    ) / total_rows
    combined = coefficient_tree(full_gram, start_merge, rank_size, freq_count)
    shifted = jnp.take(combined.reshape(freq_count, rank_size, rank_size), source, axis=0)
    result = jnp.dot(shifted.reshape(freq_count * rank_size, rank_size).T, stacked, precision=HIGH)
    return result


def solution(mesh):
    in_specs = (
        P("rows", "freq"),
        P("rows", None),
        P("rows", None, None, None),
        P("freq", None),
        P(),
    )
    out_specs = P(None, ("rows", "freq"))
    return jax.shard_map(shards, mesh=mesh, in_specs=in_specs, out_specs=out_specs, check_vma=False)
```
